768 devices in a mesh: ctx: 128 (over y, x, z_hi, core), fsdp: 6 (over z_lo).
Axes of the slice: x: 4, y: 8, z: 12 (z_hi: 2, z_lo: 6; z = z_hi * 6 + z_lo), core: 2. Of those that a mesh axis runs over, the one named last changes fastest.
Arguments:
- query_rows: bfloat16 [98304, 4096], P(('ctx', 'fsdp')), may hold values from -40 to 40
- key_rows: bfloat16 [98304, 512], P(('ctx', 'fsdp')), may hold values from -6 to 6
- value_matrix: bfloat16 [98304, 512], P(('ctx', 'fsdp')), may hold values from -6 to 6
- out_grad: bfloat16 [98304, 4096], P(('ctx', 'fsdp')), may hold values from -24 to 24
- segments: int32 [98304], P(('ctx', 'fsdp')), may hold values from 0 to 127, never falling along the last dimension, each value on 1 to 1536 neighbouring positions
Outputs:
- query_grad: bfloat16 [98304, 4096], P(('ctx', 'fsdp'))
- key_grad: bfloat16 [98304, 512], P(('ctx', 'fsdp'))
- value_grad: bfloat16 [98304, 512], P(('ctx', 'fsdp'))
The draws below stay inside these ranges and needn't reach their ends.
Inputs may be any that keep to these rules, and one draw needn't show every extreme that they name: `segments`: segment numbers never fall along the sequence.
All inputs are finite; a program needn't handle non-finite values.
Results may differ from the reference program's by a relative error of at most 0.0085.
Values may be sent and summed in bfloat16 or wider, within the bound.
No kernel may reach another device: no remote copies, remote signals or barrier semaphores. Data moves between devices by JAX's collectives and lax.ppermute only.
A program may use at most 64 MiB of HBM per device.

```python
import math
import jax
import jax.numpy as jnp
import numpy as np
from jax import lax

HEAD_WIDTH = 128
QUERY_HEADS = 32
KEY_VALUE_HEADS = 4
TOK_DEV = 128
WIN = 384
TOKEN_COUNT = 98304


def starting_keys(key):
    sender_index = jax.random.fold_in(key, 101)
    unscaled_input = jnp.clip(jax.random.normal(sender_index, (TOKEN_COUNT, KEY_VALUE_HEADS * HEAD_WIDTH), jnp.float32), -5.0, 5.0)
    return unscaled_input


def draw_key_rows(key, part):
    return starting_keys(key).astype(jnp.bfloat16)


def draw_query_rows(key, part):
    sender_index = jax.random.fold_in(key, 202)
    unscaled_input = jnp.clip(jax.random.normal(sender_index, (TOKEN_COUNT, QUERY_HEADS * HEAD_WIDTH), jnp.float32), -5.0, 5.0)
    return unscaled_input.astype(jnp.bfloat16)


def block_scale(key, dims, cuts, low, largest):
    def one(position, blocks):
        steps = jax.random.uniform(jax.random.fold_in(jax.random.fold_in(key, 6), position), (blocks,), jnp.float32, low / len(cuts), largest / len(cuts))
        return jnp.repeat(jnp.exp(steps), dims[position] // blocks).reshape((-1,) + (1,) * (len(dims) - position - 1))

    factor_of = one(*cuts[0])
    for cut in cuts[1:]:
        factor_of = factor_of * one(*cut)
    return factor_of


def split_up(count, total, limit, lean):
    loads = [(1 << 20) // math.isqrt(rank ** lean) + 1 for rank in range(2, count + 1)]
    rest, holding = total - limit - (count - 1), [1] * (count - 1)
    while rest > 0:
        movable = [i for i in range(count - 1) if holding[i] < limit]
        mass, left = sum([loads[i] for i in movable]), rest
        for i in movable:
            more = min(limit - holding[i], max(1, left * loads[i] // mass), rest)
            holding[i] = holding[i] + more
            rest = rest - more
    return np.array([limit] + holding)


def uneven(key, count, total, limit, slope):
    if count == 2:
        one = jax.random.randint(key, (), max(1, total - limit), min(limit, total - 1) + 1)
        return jnp.stack([one, total - one])
    tallies = jnp.asarray(split_up(count, total, limit, slope), jnp.int32)
    pairs = (count - 1) // 2
    source_of, receiver = tallies[1:1 + 2 * pairs:2], tallies[2:2 + 2 * pairs:2]
    room = jnp.minimum(source_of - 1, limit - receiver)
    moved = jax.random.randint(jax.random.fold_in(key, 1), (pairs,), 0, 1 << 20) % (room + 1)
    tallies = tallies.at[1:1 + 2 * pairs:2].set(source_of - moved).at[2:2 + 2 * pairs:2].set(receiver + moved)
    return tallies[jax.random.permutation(jax.random.fold_in(key, 2), count)]


def bell_draw(stream_key, extent, width, reach, split=(), kind=jnp.bfloat16):
    entries = jax.random.normal(stream_key, extent, jnp.float32) * width
    if len(split) > 0:
        entries = block_scale(stream_key, extent, split, -0.22, 0.18) * entries
    return jnp.clip(entries, min=-reach, max=reach).astype(kind)


def setup_inputs(seed: int = 0) -> dict:
    arg_keys = jax.random.split(jax.random.key(seed), 6)
    return {
        "query_rows": draw_query_rows(jax.random.fold_in(arg_keys[5], 71), 0),
        "key_rows": draw_key_rows(jax.random.fold_in(arg_keys[5], 71), 0),
        "value_matrix": bell_draw(arg_keys[2], (TOKEN_COUNT, KEY_VALUE_HEADS * HEAD_WIDTH), 1.0, 6.0, ((0, 768),)),
        "out_grad": bell_draw(arg_keys[3], (TOKEN_COUNT, QUERY_HEADS * HEAD_WIDTH), 4.0, 24.0, ((0, 768),)),
        "segments": jnp.searchsorted(jnp.cumsum(uneven(arg_keys[4], TOKEN_COUNT // (2 * WIN), TOKEN_COUNT, 4 * WIN, 2)), jnp.arange(TOKEN_COUNT), side="right").astype(jnp.int32),
    }


def band_grads(query_blk, grad_blk, key_win, value_win, query_seg, key_seg, query_first, key_first, window):
    tok_rows = query_blk.shape[0]
    key_count = key_win.shape[0]
    kv_heads = key_win.shape[1] // HEAD_WIDTH
    heads_per_group = query_blk.shape[1] // key_win.shape[1]
    inv_root = 1.0 / math.sqrt(HEAD_WIDTH)
    query_pos = query_first + jnp.arange(tok_rows, dtype=jnp.int32)
    key_pos = key_first + jnp.arange(key_count, dtype=jnp.int32)
    allowed = (key_pos[None, :] > query_pos[:, None] - window) & (key_pos[None, :] <= query_pos[:, None])
    allowed = allowed & (key_pos[None, :] >= 0) & (key_seg[None, :] == query_seg[:, None])
    query_parts = []
    key_parts = []
    value_parts = []
    for kv_head in range(kv_heads):
        k_head = key_win[:, kv_head * HEAD_WIDTH:(kv_head + 1) * HEAD_WIDTH].astype(jnp.float32)
        v_head = value_win[:, kv_head * HEAD_WIDTH:(kv_head + 1) * HEAD_WIDTH].astype(jnp.float32)
        lower = kv_head * heads_per_group * HEAD_WIDTH
        q_head = query_blk[:, lower:lower + heads_per_group * HEAD_WIDTH].reshape(tok_rows, heads_per_group, HEAD_WIDTH).astype(jnp.float32)
        o_grad = grad_blk[:, lower:lower + heads_per_group * HEAD_WIDTH].reshape(tok_rows, heads_per_group, HEAD_WIDTH).astype(jnp.float32)
        scores = jnp.einsum('trd,kd->rtk', q_head, k_head) * inv_root
        scores = jnp.where(allowed[None], scores, -1e+30)
        row_max = lax.optimization_barrier(jnp.max(scores, axis=-1, keepdims=True))
        weights = jnp.exp(scores - row_max)
        probs = weights / lax.optimization_barrier(jnp.sum(weights, axis=-1, keepdims=True))
        prob_grad = jnp.einsum('trd,kd->rtk', o_grad, v_head)
        row_delta = lax.optimization_barrier(jnp.sum(probs * prob_grad, axis=-1, keepdims=True))
        score_grad = lax.optimization_barrier((probs * (prob_grad - row_delta) * inv_root).astype(jnp.bfloat16)).astype(jnp.float32)
        probs_low = lax.optimization_barrier(probs.astype(jnp.bfloat16)).astype(jnp.float32)
        query_parts.append(jnp.einsum('rtk,kd->trd', score_grad, k_head).reshape(tok_rows, heads_per_group * HEAD_WIDTH))
        key_parts.append(jnp.einsum('rtk,trd->kd', score_grad, q_head))
        value_parts.append(jnp.einsum('rtk,trd->kd', probs_low, o_grad))
    return (jnp.concatenate(query_parts, 1), jnp.concatenate(key_parts, 1), jnp.concatenate(value_parts, 1))

def reference(query_rows, key_rows, value_matrix, out_grad, segments):
    block_count = TOKEN_COUNT // TOK_DEV
    key_count = WIN + TOK_DEV
    kv_width = key_rows.shape[1]
    key_padded = jnp.concatenate([jnp.zeros((WIN, kv_width), key_rows.dtype), key_rows], 0)
    value_padded = jnp.concatenate([jnp.zeros((WIN, kv_width), value_matrix.dtype), value_matrix], 0)
    seg_padded = jnp.concatenate([-jnp.ones((WIN,), jnp.int32), segments.astype(jnp.int32)], 0)

    def advance(carry, block_index):
        key_acc, value_acc = carry
        query_first = (block_index * TOK_DEV).astype(jnp.int32)
        query_blk = lax.dynamic_slice_in_dim(query_rows, query_first, TOK_DEV, 0)
        grad_blk = lax.dynamic_slice_in_dim(out_grad, query_first, TOK_DEV, 0)
        query_seg = lax.dynamic_slice_in_dim(segments.astype(jnp.int32), query_first, TOK_DEV, 0)
        key_win = lax.dynamic_slice_in_dim(key_padded, query_first, key_count, 0)
        value_win = lax.dynamic_slice_in_dim(value_padded, query_first, key_count, 0)
        key_seg = lax.dynamic_slice_in_dim(seg_padded, query_first, key_count, 0)
        dq_part, dk_part, dv_part = band_grads(query_blk, grad_blk, key_win, value_win, query_seg, key_seg, query_first, query_first - WIN, WIN)
        key_acc = lax.dynamic_update_slice_in_dim(key_acc, lax.dynamic_slice_in_dim(key_acc, query_first, key_count, 0) + dk_part, query_first, 0)
        value_acc = lax.dynamic_update_slice_in_dim(value_acc, lax.dynamic_slice_in_dim(value_acc, query_first, key_count, 0) + dv_part, query_first, 0)
        return ((key_acc, value_acc), dq_part.astype(jnp.bfloat16))
    zeros = jnp.zeros((TOKEN_COUNT + WIN, kv_width), jnp.float32)
    (key_acc, value_acc), dq_blocks = lax.scan(advance, (zeros, zeros), jnp.arange(block_count, dtype=jnp.int32))
    query_grad = dq_blocks.reshape(TOKEN_COUNT, dq_blocks.shape[2])
    return (query_grad, key_acc[WIN:].astype(jnp.bfloat16), value_acc[WIN:].astype(jnp.bfloat16))
```

```python
import math

import jax
import jax.numpy as jnp
from jax import lax
from jax.sharding import PartitionSpec as P

HEAD_WIDTH = 128
SPAN = 3


def from_behind(block, axis, distance):
    devices = range(lax.axis_size(axis))
    route = [(i - distance, i) for i in devices if i - distance in devices]
    return lax.ppermute(block, axis, route)


def band_grads(
    query_blk, grad_blk, key_win, value_win, query_seg, key_seg, query_first, key_first, window
):
    tok_rows = query_blk.shape[0]
    key_count = key_win.shape[0]
    kv_heads = key_win.shape[1] // HEAD_WIDTH
    heads_per_group = query_blk.shape[1] // key_win.shape[1]
    inv_root = 1.0 / math.sqrt(HEAD_WIDTH)
    query_pos = query_first + jnp.arange(tok_rows, dtype=jnp.int32)
    key_pos = key_first + jnp.arange(key_count, dtype=jnp.int32)
    allowed = (key_pos[None, :] > query_pos[:, None] - window) & (
        key_pos[None, :] <= query_pos[:, None]
    )
    allowed = allowed & (key_pos[None, :] >= 0) & (key_seg[None, :] == query_seg[:, None])
    query_parts = []
    key_parts = []
    value_parts = []
    for kv_head in range(kv_heads):
        k_head = key_win[:, kv_head * HEAD_WIDTH : (kv_head + 1) * HEAD_WIDTH]
        v_head = value_win[:, kv_head * HEAD_WIDTH : (kv_head + 1) * HEAD_WIDTH]
        lower = kv_head * heads_per_group * HEAD_WIDTH
        q_head = query_blk[:, lower : lower + heads_per_group * HEAD_WIDTH].reshape(
            tok_rows, heads_per_group, HEAD_WIDTH
        )
        o_grad = grad_blk[:, lower : lower + heads_per_group * HEAD_WIDTH].reshape(
            tok_rows, heads_per_group, HEAD_WIDTH
        )
        scores = (
            jnp.einsum("trd,kd->rtk", q_head, k_head, preferred_element_type=jnp.float32) * inv_root
        )
        scores = jnp.where(allowed[None], scores, -1e30)
        row_max = jnp.max(scores, axis=-1, keepdims=True)
        weights = jnp.exp(scores - row_max)
        probs = weights / jnp.sum(weights, axis=-1, keepdims=True)
        prob_grad = jnp.einsum("trd,kd->rtk", o_grad, v_head, preferred_element_type=jnp.float32)
        row_delta = jnp.sum(probs * prob_grad, axis=-1, keepdims=True)
        score_grad = (probs * (prob_grad - row_delta) * inv_root).astype(jnp.bfloat16)
        probs_low = probs.astype(jnp.bfloat16)
        query_parts.append(
            jnp.einsum(
                "rtk,kd->trd", score_grad, k_head, preferred_element_type=jnp.float32
            ).reshape(tok_rows, heads_per_group * HEAD_WIDTH)
        )
        key_parts.append(
            jnp.einsum("rtk,trd->kd", score_grad, q_head, preferred_element_type=jnp.float32)
        )
        value_parts.append(
            jnp.einsum("rtk,trd->kd", probs_low, o_grad, preferred_element_type=jnp.float32)
        )
    return (
        jnp.concatenate(query_parts, 1),
        jnp.concatenate(key_parts, 1),
        jnp.concatenate(value_parts, 1),
    )


def body(query_rows, key_rows, value_matrix, out_grad, segments):
    tok_rows = query_rows.shape[0]
    kv_width = key_rows.shape[1]
    position = lax.axis_index(("ctx", "fsdp"))
    query_first = position * tok_rows
    window = SPAN * tok_rows
    pair = jnp.concatenate([key_rows, value_matrix], 1)
    nearby = [(pair, segments)]
    for hop_back in range(1, SPAN + 1):
        nearby.insert(0, from_behind(nearby[0], ("ctx", "fsdp"), 1))
    pair_win = jnp.concatenate([member[0] for member in nearby], 0)
    seg_win = jnp.concatenate([member[1] for member in nearby], 0)
    dq_part, dk_part, dv_part = band_grads(
        query_rows,
        out_grad,
        pair_win[:, :kv_width],
        pair_win[:, kv_width:],
        segments,
        seg_win,
        query_first,
        query_first - window,
        window,
    )
    grad_part = jnp.concatenate([dk_part, dv_part], 1)
    carried = grad_part[:tok_rows]
    for relay_step in range(1, SPAN + 1):
        received = from_behind(carried.astype(jnp.bfloat16), ("ctx", "fsdp"), -1)
        lower = relay_step * tok_rows
        carried = received.astype(jnp.float32) + grad_part[lower : lower + tok_rows]
    return (
        dq_part.astype(jnp.bfloat16),
        carried[:, :kv_width].astype(jnp.bfloat16),
        carried[:, kv_width:].astype(jnp.bfloat16),
    )


def solution(mesh):
    return jax.shard_map(
        body,
        mesh=mesh,
        in_specs=(
            P(("ctx", "fsdp"), None),
            P(("ctx", "fsdp"), None),
            P(("ctx", "fsdp"), None),
            P(("ctx", "fsdp"), None),
            P(("ctx", "fsdp")),
        ),
        out_specs=(P(("ctx", "fsdp"), None), P(("ctx", "fsdp"), None), P(("ctx", "fsdp"), None)),
        check_vma=False,
    )
```

```python
import math

import jax
import jax.numpy as jnp
from jax import lax
from jax.experimental import pallas as pl
from jax.sharding import PartitionSpec as P

HEAD_WIDTH = 128
SPAN = 3


def from_behind(block, axis, distance):
    devices = range(lax.axis_size(axis))
    route = [(i - distance, i) for i in devices if i - distance in devices]
    return lax.ppermute(block, axis, route)


def band_kernel(seg_q_ref, seg_k_ref, query_ref, grad_ref, pair_ref, dq_ref, dpair_ref):
    tok_rows = query_ref.shape[0]
    key_count = pair_ref.shape[0]
    heads_per_group = query_ref.shape[1] // HEAD_WIDTH
    inv_root = 1.0 / math.sqrt(HEAD_WIDTH)
    row = lax.broadcasted_iota(jnp.int32, (tok_rows, key_count), 0)
    col = lax.broadcasted_iota(jnp.int32, (tok_rows, key_count), 1)
    window = key_count - tok_rows
    allowed = (col > row) & (col <= row + window) & (seg_k_ref[...] == seg_q_ref[...])
    k_head = pair_ref[:, :HEAD_WIDTH]
    v_head = pair_ref[:, HEAD_WIDTH:]
    key_acc = jnp.zeros((key_count, HEAD_WIDTH), jnp.float32)
    value_acc = jnp.zeros((key_count, HEAD_WIDTH), jnp.float32)
    for head in range(heads_per_group):
        cols = slice(head * HEAD_WIDTH, (head + 1) * HEAD_WIDTH)
        q_head = query_ref[:, cols]
        o_grad = grad_ref[:, cols]
        scores = lax.dot_general(
            q_head, k_head, (((1,), (1,)), ((), ())), preferred_element_type=jnp.float32
        )
        scores = jnp.where(allowed, scores * inv_root, -1e30)
        row_max = jnp.max(scores, axis=1, keepdims=True)
        weights = jnp.exp(scores - row_max)
        probs = weights * (1.0 / jnp.sum(weights, axis=1, keepdims=True))
        prob_grad = lax.dot_general(
            o_grad, v_head, (((1,), (1,)), ((), ())), preferred_element_type=jnp.float32
        )
        row_delta = jnp.sum(probs * prob_grad, axis=1, keepdims=True)
        score_grad = (probs * (prob_grad - row_delta) * inv_root).astype(jnp.bfloat16)
        probs_low = probs.astype(jnp.bfloat16)
        dq_ref[:, cols] = jnp.dot(
            score_grad, k_head, preferred_element_type=jnp.float32
        ).astype(jnp.bfloat16)
        key_acc = key_acc + lax.dot_general(
            score_grad, q_head, (((0,), (0,)), ((), ())), preferred_element_type=jnp.float32
        )
        value_acc = value_acc + lax.dot_general(
            probs_low, o_grad, (((0,), (0,)), ((), ())), preferred_element_type=jnp.float32
        )
    dpair_ref[:, :HEAD_WIDTH] = key_acc
    dpair_ref[:, HEAD_WIDTH:] = value_acc


def band_grads(query_blk, grad_blk, pair_win, query_seg, key_seg):
    tok_rows, q_width = query_blk.shape
    key_count, pair_width = pair_win.shape
    kv_heads = pair_width // (2 * HEAD_WIDTH)
    group_width = q_width // kv_heads
    return pl.pallas_call(
        band_kernel,
        grid=(kv_heads,),
        in_specs=[
            pl.BlockSpec((tok_rows, 1), lambda g: (0, 0)),
            pl.BlockSpec((1, key_count), lambda g: (0, 0)),
            pl.BlockSpec((tok_rows, group_width), lambda g: (0, g)),
            pl.BlockSpec((tok_rows, group_width), lambda g: (0, g)),
            pl.BlockSpec((key_count, 2 * HEAD_WIDTH), lambda g: (0, g)),
        ],
        out_specs=[
            pl.BlockSpec((tok_rows, group_width), lambda g: (0, g)),
            pl.BlockSpec((key_count, 2 * HEAD_WIDTH), lambda g: (0, g)),
        ],
        out_shape=[
            jax.ShapeDtypeStruct((tok_rows, q_width), jnp.bfloat16),
            jax.ShapeDtypeStruct((key_count, pair_width), jnp.float32),
        ],
    )(query_seg.reshape(tok_rows, 1), key_seg.reshape(1, key_count), query_blk, grad_blk, pair_win)


def interleave(first, second):
    rows, width = first.shape
    heads = width // HEAD_WIDTH
    return jnp.stack(
        [first.reshape(rows, heads, HEAD_WIDTH), second.reshape(rows, heads, HEAD_WIDTH)], 2
    ).reshape(rows, 2 * width)


def body(query_rows, key_rows, value_matrix, out_grad, segments):
    tok_rows = query_rows.shape[0]
    kv_width = key_rows.shape[1]
    position = lax.axis_index(("ctx", "fsdp"))
    query_first = position * tok_rows
    window = SPAN * tok_rows
    pair = interleave(key_rows, value_matrix)
    nearby = [(pair, segments)]
    for hop_back in range(1, SPAN + 1):
        nearby.insert(0, from_behind(nearby[0], ("ctx", "fsdp"), 1))
    pair_win = jnp.concatenate([member[0] for member in nearby], 0)
    seg_win = jnp.concatenate([member[1] for member in nearby], 0)
    key_pos = query_first - window + jnp.arange(window + tok_rows, dtype=jnp.int32)
    seg_win = jnp.where(key_pos >= 0, seg_win, -1)
    dq_part, grad_part = band_grads(query_rows, out_grad, pair_win, segments, seg_win)
    carried = grad_part[:tok_rows]
    for relay_step in range(1, SPAN + 1):
        received = from_behind(carried.astype(jnp.bfloat16), ("ctx", "fsdp"), -1)
        lower = relay_step * tok_rows
        carried = received.astype(jnp.float32) + grad_part[lower : lower + tok_rows]
    carried = carried.reshape(tok_rows, kv_width // HEAD_WIDTH, 2, HEAD_WIDTH)
    return (
        dq_part,
        carried[:, :, 0].reshape(tok_rows, kv_width).astype(jnp.bfloat16),
        carried[:, :, 1].reshape(tok_rows, kv_width).astype(jnp.bfloat16),
    )


def solution(mesh):
    return jax.shard_map(
        body,
        mesh=mesh,
        in_specs=(
            P(("ctx", "fsdp"), None),
            P(("ctx", "fsdp"), None),
            P(("ctx", "fsdp"), None),
            P(("ctx", "fsdp"), None),
            P(("ctx", "fsdp")),
        ),
        out_specs=(P(("ctx", "fsdp"), None), P(("ctx", "fsdp"), None), P(("ctx", "fsdp"), None)),
        check_vma=False,
    )
```

```python
import math

import jax
import jax.numpy as jnp
from jax import lax
from jax.experimental import pallas as pl
from jax.sharding import PartitionSpec as P

HEAD_WIDTH = 128
SPAN = 3


def from_behind(block, axis, distance):
    devices = range(lax.axis_size(axis))
    route = [(i - distance, i) for i in devices if i - distance in devices]
    return lax.ppermute(block, axis, route)


def band_kernel(seg_q_ref, seg_k_ref, query_ref, grad_ref, *refs):
    key_refs = refs[0:8:2]
    value_refs = refs[1:8:2]
    dq_ref, send_ref, middle_ref, own_ref = refs[8:]
    tok_rows = query_ref.shape[0]
    key_count = tok_rows * len(key_refs)
    heads_per_group = query_ref.shape[1] // HEAD_WIDTH
    inv_root = 1.0 / math.sqrt(HEAD_WIDTH)
    row = lax.broadcasted_iota(jnp.int32, (tok_rows, key_count), 0)
    col = lax.broadcasted_iota(jnp.int32, (tok_rows, key_count), 1)
    window = key_count - tok_rows
    allowed = (col > row) & (col <= row + window) & (seg_k_ref[...] == seg_q_ref[...])
    k_head = jnp.concatenate([ref[...] for ref in key_refs], 0)
    v_head = jnp.concatenate([ref[...] for ref in value_refs], 0)
    key_acc = jnp.zeros((key_count, HEAD_WIDTH), jnp.float32)
    value_acc = jnp.zeros((key_count, HEAD_WIDTH), jnp.float32)
    for head in range(heads_per_group):
        cols = slice(head * HEAD_WIDTH, (head + 1) * HEAD_WIDTH)
        q_head = query_ref[:, cols]
        o_grad = grad_ref[:, cols]
        scores = lax.dot_general(
            q_head, k_head, (((1,), (1,)), ((), ())), preferred_element_type=jnp.float32
        )
        scores = jnp.where(allowed, scores * inv_root, -1e30)
        row_max = jnp.max(scores, axis=1, keepdims=True)
        weights = jnp.exp(scores - row_max)
        probs = weights * (1.0 / jnp.sum(weights, axis=1, keepdims=True))
        prob_grad = lax.dot_general(
            o_grad, v_head, (((1,), (1,)), ((), ())), preferred_element_type=jnp.float32
        )
        row_delta = jnp.sum(probs * prob_grad, axis=1, keepdims=True)
        score_grad = (probs * (prob_grad - row_delta) * inv_root).astype(jnp.bfloat16)
        probs_low = probs.astype(jnp.bfloat16)
        dq_ref[:, cols] = jnp.dot(
            score_grad, k_head, preferred_element_type=jnp.float32
        ).astype(jnp.bfloat16)
        key_acc = key_acc + lax.dot_general(
            score_grad, q_head, (((0,), (0,)), ((), ())), preferred_element_type=jnp.float32
        )
        value_acc = value_acc + lax.dot_general(
            probs_low, o_grad, (((0,), (0,)), ((), ())), preferred_element_type=jnp.float32
        )

    def rows(block):
        return slice(block * tok_rows, (block + 1) * tok_rows)

    w = HEAD_WIDTH
    send_ref[:, 0:w] = key_acc[rows(0)].astype(jnp.bfloat16)
    send_ref[:, w : 2 * w] = value_acc[rows(0)].astype(jnp.bfloat16)
    send_ref[:, 2 * w : 3 * w] = key_acc[rows(2)].astype(jnp.bfloat16)
    send_ref[:, 3 * w : 4 * w] = value_acc[rows(2)].astype(jnp.bfloat16)
    middle_ref[:, 0:w] = key_acc[rows(1)]
    middle_ref[:, w : 2 * w] = value_acc[rows(1)]
    own_ref[:, 0:w] = key_acc[rows(3)]
    own_ref[:, w : 2 * w] = value_acc[rows(3)]


def band_grads(query_blk, grad_blk, blocks, query_seg, key_seg):
    tok_rows, q_width = query_blk.shape
    kv_heads = (blocks[0].shape[1] - HEAD_WIDTH) // (2 * HEAD_WIDTH)
    group_width = q_width // kv_heads
    kv_specs = []
    kv_args = []
    for blk in blocks:
        kv_specs.append(pl.BlockSpec((tok_rows, HEAD_WIDTH), lambda g: (0, g)))
        kv_specs.append(pl.BlockSpec((tok_rows, HEAD_WIDTH), lambda g, n=kv_heads: (0, n + g)))
        kv_args += [blk, blk]
    return pl.pallas_call(
        band_kernel,
        grid=(kv_heads,),
        in_specs=[
            pl.BlockSpec((tok_rows, 1), lambda g: (0, 0)),
            pl.BlockSpec((1, key_seg.shape[0]), lambda g: (0, 0)),
            pl.BlockSpec((tok_rows, group_width), lambda g: (0, g)),
            pl.BlockSpec((tok_rows, group_width), lambda g: (0, g)),
        ]
        + kv_specs,
        out_specs=[
            pl.BlockSpec((tok_rows, group_width), lambda g: (0, g)),
            pl.BlockSpec((tok_rows, 4 * HEAD_WIDTH), lambda g: (0, g)),
            pl.BlockSpec((tok_rows, 2 * HEAD_WIDTH), lambda g: (0, g)),
            pl.BlockSpec((tok_rows, 2 * HEAD_WIDTH), lambda g: (0, g)),
        ],
        out_shape=[
            jax.ShapeDtypeStruct((tok_rows, q_width), jnp.bfloat16),
            jax.ShapeDtypeStruct((tok_rows, 4 * HEAD_WIDTH * kv_heads), jnp.bfloat16),
            jax.ShapeDtypeStruct((tok_rows, 2 * HEAD_WIDTH * kv_heads), jnp.float32),
            jax.ShapeDtypeStruct((tok_rows, 2 * HEAD_WIDTH * kv_heads), jnp.float32),
        ],
    )(query_seg.reshape(tok_rows, 1), key_seg.reshape(1, -1), query_blk, grad_blk, *kv_args)


def body(query_rows, key_rows, value_matrix, out_grad, segments):
    tok_rows = query_rows.shape[0]
    kv_width = key_rows.shape[1]
    kv_heads = kv_width // HEAD_WIDTH
    axes = ("ctx", "fsdp")
    position = lax.axis_index(axes)
    query_first = position * tok_rows
    window = SPAN * tok_rows
    seg_cols = jnp.broadcast_to(segments.astype(jnp.bfloat16)[:, None], (tok_rows, HEAD_WIDTH))
    own = jnp.concatenate([key_rows, value_matrix, seg_cols], 1)
    back_one = from_behind(own, axes, 1)
    back_two = from_behind(own, axes, 2)
    back_three = from_behind(back_two, axes, 1)
    blocks = [back_three, back_two, back_one, own]
    seg_win = jnp.concatenate([blk[:, 2 * kv_width] for blk in blocks], 0).astype(jnp.int32)
    key_pos = query_first - window + jnp.arange(window + tok_rows, dtype=jnp.int32)
    seg_win = jnp.where(key_pos >= 0, seg_win, -1)
    dq_part, send, middle, own_part = band_grads(query_rows, out_grad, blocks, segments, seg_win)
    received = from_behind(send, axes, -1).reshape(tok_rows, kv_heads, 2, 2 * HEAD_WIDTH)
    middle = middle.reshape(tok_rows, kv_heads, 2 * HEAD_WIDTH)
    forward = (middle + received[:, :, 0].astype(jnp.float32)).astype(jnp.bfloat16)
    gathered = from_behind(forward, axes, -2)
    total = (
        own_part.reshape(tok_rows, kv_heads, 2 * HEAD_WIDTH)
        + received[:, :, 1].astype(jnp.float32)
        + gathered.astype(jnp.float32)
    ).reshape(tok_rows, kv_heads, 2, HEAD_WIDTH)
    return (
        dq_part,
        total[:, :, 0].reshape(tok_rows, kv_width).astype(jnp.bfloat16),
        total[:, :, 1].reshape(tok_rows, kv_width).astype(jnp.bfloat16),
    )


def solution(mesh):
    return jax.shard_map(
        body,
        mesh=mesh,
        in_specs=(
            P(("ctx", "fsdp"), None),
            P(("ctx", "fsdp"), None),
            P(("ctx", "fsdp"), None),
            P(("ctx", "fsdp"), None),
            P(("ctx", "fsdp")),
        ),
        out_specs=(P(("ctx", "fsdp"), None), P(("ctx", "fsdp"), None), P(("ctx", "fsdp"), None)),
        check_vma=False,
    )
```

```python
import math

import jax
import jax.numpy as jnp
from jax import lax
from jax.experimental import pallas as pl
from jax.sharding import PartitionSpec as P

HEAD_WIDTH = 128
SPAN = 3
GROUP_HEADS = 8


def from_behind(block, axis, distance):
    devices = range(lax.axis_size(axis))
    route = [(i - distance, i) for i in devices if i - distance in devices]
    return lax.ppermute(block, axis, route)


def band_kernel(seg_q_ref, seg_k_ref, query_ref, grad_ref, *refs):
    key_refs = refs[0:8:2]
    value_refs = refs[1:8:2]
    dq_ref, send_ref, middle_ref, own_ref = refs[-4:]
    tok_rows = query_ref.shape[0]
    key_count = tok_rows * len(key_refs)
    heads_per_group = query_ref.shape[1] // HEAD_WIDTH
    inv_root = 1.0 / math.sqrt(HEAD_WIDTH)
    row = lax.broadcasted_iota(jnp.int32, (tok_rows, key_count), 0)
    col = lax.broadcasted_iota(jnp.int32, (tok_rows, key_count), 1)
    window = key_count - tok_rows
    allowed = (col > row) & (col <= row + window) & (seg_k_ref[...] == seg_q_ref[...])
    k_head = jnp.concatenate([ref[...] for ref in key_refs], 0)
    v_head = jnp.concatenate([ref[...] for ref in value_refs], 0)
    key_acc = jnp.zeros((key_count, HEAD_WIDTH), jnp.float32)
    value_acc = jnp.zeros((key_count, HEAD_WIDTH), jnp.float32)
    for head in range(heads_per_group):
        cols = slice(head * HEAD_WIDTH, (head + 1) * HEAD_WIDTH)
        q_head = query_ref[:, cols]
        o_grad = grad_ref[:, cols]
        scores = lax.dot_general(
            q_head, k_head, (((1,), (1,)), ((), ())), preferred_element_type=jnp.float32
        )
        scores = jnp.where(allowed, scores * inv_root, -1e30)
        row_max = jnp.max(scores, axis=1, keepdims=True)
        weights = jnp.exp(scores - row_max)
        probs = weights * (1.0 / jnp.sum(weights, axis=1, keepdims=True))
        prob_grad = lax.dot_general(
            o_grad, v_head, (((1,), (1,)), ((), ())), preferred_element_type=jnp.float32
        )
        row_delta = jnp.sum(probs * prob_grad, axis=1, keepdims=True)
        score_grad = (probs * (prob_grad - row_delta) * inv_root).astype(jnp.bfloat16)
        probs_low = probs.astype(jnp.bfloat16)
        dq_ref[:, cols] = jnp.dot(
            score_grad, k_head, preferred_element_type=jnp.float32
        ).astype(jnp.bfloat16)
        key_acc = key_acc + lax.dot_general(
            score_grad, q_head, (((0,), (0,)), ((), ())), preferred_element_type=jnp.float32
        )
        value_acc = value_acc + lax.dot_general(
            probs_low, o_grad, (((0,), (0,)), ((), ())), preferred_element_type=jnp.float32
        )

    def rows(block):
        return slice(block * tok_rows, (block + 1) * tok_rows)

    w = HEAD_WIDTH
    send_ref[:, 0:w] = key_acc[rows(0)].astype(jnp.bfloat16)
    send_ref[:, w : 2 * w] = value_acc[rows(0)].astype(jnp.bfloat16)
    send_ref[:, 2 * w : 3 * w] = key_acc[rows(2)].astype(jnp.bfloat16)
    send_ref[:, 3 * w : 4 * w] = value_acc[rows(2)].astype(jnp.bfloat16)
    middle_ref[:, 0:w] = key_acc[rows(1)]
    middle_ref[:, w : 2 * w] = value_acc[rows(1)]
    own_ref[:, 0:w] = key_acc[rows(3)]
    own_ref[:, w : 2 * w] = value_acc[rows(3)]


def band_grads(query_rows, out_grad, blocks, query_seg, key_seg, first_kv, kv_heads, dq_buf):
    tok_rows, q_width = query_rows.shape
    group_width = HEAD_WIDTH * GROUP_HEADS
    kv_specs = []
    kv_args = []
    for blk in blocks:
        kv_specs.append(pl.BlockSpec((tok_rows, HEAD_WIDTH), lambda g: (0, g)))
        kv_specs.append(pl.BlockSpec((tok_rows, HEAD_WIDTH), lambda g, n=kv_heads: (0, n + g)))
        kv_args += [blk, blk]
    extra_specs = []
    extra_args = []
    aliases = {}
    if dq_buf is not None:
        extra_specs = [pl.BlockSpec(memory_space=pl.ANY)]
        extra_args = [dq_buf]
        aliases = {4 + len(kv_args): 0}
    return pl.pallas_call(
        band_kernel,
        grid=(kv_heads,),
        in_specs=[
            pl.BlockSpec((tok_rows, 1), lambda g: (0, 0)),
            pl.BlockSpec((1, key_seg.shape[0]), lambda g: (0, 0)),
            pl.BlockSpec((tok_rows, group_width), lambda g, f=first_kv: (0, f + g)),
            pl.BlockSpec((tok_rows, group_width), lambda g, f=first_kv: (0, f + g)),
        ]
        + kv_specs
        + extra_specs,
        out_specs=[
            pl.BlockSpec((tok_rows, group_width), lambda g, f=first_kv: (0, f + g)),
            pl.BlockSpec((tok_rows, 4 * HEAD_WIDTH), lambda g: (0, g)),
            pl.BlockSpec((tok_rows, 2 * HEAD_WIDTH), lambda g: (0, g)),
            pl.BlockSpec((tok_rows, 2 * HEAD_WIDTH), lambda g: (0, g)),
        ],
        out_shape=[
            jax.ShapeDtypeStruct((tok_rows, q_width), jnp.bfloat16),
            jax.ShapeDtypeStruct((tok_rows, 4 * HEAD_WIDTH * kv_heads), jnp.bfloat16),
            jax.ShapeDtypeStruct((tok_rows, 2 * HEAD_WIDTH * kv_heads), jnp.float32),
            jax.ShapeDtypeStruct((tok_rows, 2 * HEAD_WIDTH * kv_heads), jnp.float32),
        ],
        input_output_aliases=aliases,
    )(
        query_seg.reshape(tok_rows, 1),
        key_seg.reshape(1, -1),
        query_rows,
        out_grad,
        *kv_args,
        *extra_args,
    )


def body(query_rows, key_rows, value_matrix, out_grad, segments):
    tok_rows = query_rows.shape[0]
    kv_width = key_rows.shape[1]
    kv_heads = kv_width // HEAD_WIDTH
    halves = 2
    half_heads = kv_heads // halves
    half_width = half_heads * HEAD_WIDTH
    axes = ("ctx", "fsdp")
    position = lax.axis_index(axes)
    query_first = position * tok_rows
    window = SPAN * tok_rows
    seg_cols = jnp.broadcast_to(segments.astype(jnp.bfloat16)[:, None], (tok_rows, HEAD_WIDTH))
    dq_buf = None
    previous = None
    seg_win = None
    key_parts = []
    value_parts = []
    for half in range(halves):
        cols = slice(half * half_width, (half + 1) * half_width)
        pieces = [key_rows[:, cols], value_matrix[:, cols]]
        if half == 0:
            pieces.append(seg_cols)
        own = jnp.concatenate(pieces, 1)
        if previous is not None:
            own, previous = lax.optimization_barrier((own, previous))
        back_one = from_behind(own, axes, 1)
        back_two = from_behind(own, axes, 2)
        back_three = from_behind(back_two, axes, 1)
        blocks = [back_three, back_two, back_one, own]
        previous = blocks
        if seg_win is None:
            seg_win = jnp.concatenate([blk[:, 2 * half_width] for blk in blocks], 0)
            key_pos = query_first - window + jnp.arange(window + tok_rows, dtype=jnp.int32)
            seg_win = jnp.where(key_pos >= 0, seg_win.astype(jnp.int32), -1)
        dq_buf, send, middle, own_part = band_grads(
            query_rows, out_grad, blocks, segments, seg_win, half * half_heads, half_heads, dq_buf
        )
        received = from_behind(send, axes, -1).reshape(tok_rows, half_heads, 2, 2 * HEAD_WIDTH)
        middle = middle.reshape(tok_rows, half_heads, 2 * HEAD_WIDTH)
        forward = (middle + received[:, :, 0].astype(jnp.float32)).astype(jnp.bfloat16)
        gathered = from_behind(forward, axes, -2)
        total = (
            own_part.reshape(tok_rows, half_heads, 2 * HEAD_WIDTH)
            + received[:, :, 1].astype(jnp.float32)
            + gathered.astype(jnp.float32)
        ).reshape(tok_rows, half_heads, 2, HEAD_WIDTH)
        key_parts.append(total[:, :, 0].reshape(tok_rows, half_width).astype(jnp.bfloat16))
        value_parts.append(total[:, :, 1].reshape(tok_rows, half_width).astype(jnp.bfloat16))
    return (
        dq_buf,
        jnp.concatenate(key_parts, 1),
        jnp.concatenate(value_parts, 1),
    )


def solution(mesh):
    return jax.shard_map(
        body,
        mesh=mesh,
        in_specs=(
            P(("ctx", "fsdp"), None),
            P(("ctx", "fsdp"), None),
            P(("ctx", "fsdp"), None),
            P(("ctx", "fsdp"), None),
            P(("ctx", "fsdp")),
        ),
        out_specs=(P(("ctx", "fsdp"), None), P(("ctx", "fsdp"), None), P(("ctx", "fsdp"), None)),
        check_vma=False,
    )
```

```python
import math

import jax
import jax.numpy as jnp
from jax import lax
from jax.experimental import pallas as pl
from jax.sharding import PartitionSpec as P

HEAD_WIDTH = 128
SPAN = 3


def from_behind(block, axis, distance):
    devices = range(lax.axis_size(axis))
    route = [(i - distance, i) for i in devices if i - distance in devices]
    return lax.ppermute(block, axis, route)


def band_kernel(query_ref, grad_ref, *refs):
    key_refs = refs[0:12:3]
    value_refs = refs[1:12:3]
    seg_refs = refs[2:12:3]
    dq_ref, send_ref, middle_ref, own_ref = refs[12:]
    tok_rows = query_ref.shape[0]
    key_count = tok_rows * len(key_refs)
    heads_per_group = query_ref.shape[1] // HEAD_WIDTH
    inv_root = 1.0 / math.sqrt(HEAD_WIDTH)
    window = key_count - tok_rows
    position = lax.axis_index(("ctx", "fsdp"))
    seg_q = seg_refs[-1][:, 0:1].astype(jnp.float32)
    seg_k = jnp.concatenate(
        [jnp.transpose(ref[...].astype(jnp.float32))[0:1] for ref in seg_refs], 1
    )
    row = lax.broadcasted_iota(jnp.int32, (tok_rows, key_count), 0)
    col = lax.broadcasted_iota(jnp.int32, (tok_rows, key_count), 1)
    allowed = (col > row) & (col <= row + window) & (col >= window - position * tok_rows)
    allowed = allowed & (seg_k == seg_q)
    k_head = jnp.concatenate([ref[...] for ref in key_refs], 0)
    v_head = jnp.concatenate([ref[...] for ref in value_refs], 0)
    key_acc = jnp.zeros((key_count, HEAD_WIDTH), jnp.float32)
    value_acc = jnp.zeros((key_count, HEAD_WIDTH), jnp.float32)
    for head in range(heads_per_group):
        cols = slice(head * HEAD_WIDTH, (head + 1) * HEAD_WIDTH)
        q_head = query_ref[:, cols]
        o_grad = grad_ref[:, cols]
        scores = lax.dot_general(
            q_head, k_head, (((1,), (1,)), ((), ())), preferred_element_type=jnp.float32
        )
        scores = jnp.where(allowed, scores * inv_root, -1e30)
        row_max = jnp.max(scores, axis=1, keepdims=True)
        weights = jnp.exp(scores - row_max)
        probs = weights * (1.0 / jnp.sum(weights, axis=1, keepdims=True))
        prob_grad = lax.dot_general(
            o_grad, v_head, (((1,), (1,)), ((), ())), preferred_element_type=jnp.float32
        )
        row_delta = jnp.sum(probs * prob_grad, axis=1, keepdims=True)
        score_grad = (probs * (prob_grad - row_delta) * inv_root).astype(jnp.bfloat16)
        probs_low = probs.astype(jnp.bfloat16)
        dq_ref[:, cols] = jnp.dot(
            score_grad, k_head, preferred_element_type=jnp.float32
        ).astype(jnp.bfloat16)
        key_acc = key_acc + lax.dot_general(
            score_grad, q_head, (((0,), (0,)), ((), ())), preferred_element_type=jnp.float32
        )
        value_acc = value_acc + lax.dot_general(
            probs_low, o_grad, (((0,), (0,)), ((), ())), preferred_element_type=jnp.float32
        )

    def rows(block):
        return slice(block * tok_rows, (block + 1) * tok_rows)

    for slot, block in enumerate((0, 2)):
        send_ref[slot, 0] = key_acc[rows(block)].astype(jnp.bfloat16)
        send_ref[slot, 1] = value_acc[rows(block)].astype(jnp.bfloat16)
    middle_ref[0] = key_acc[rows(1)]
    middle_ref[1] = value_acc[rows(1)]
    own_ref[0] = key_acc[rows(3)]
    own_ref[1] = value_acc[rows(3)]


def band_grads(query_blk, grad_blk, blocks, kv_heads):
    tok_rows, q_width = query_blk.shape
    kv_width = kv_heads * HEAD_WIDTH
    group_width = q_width // kv_heads
    kv_specs = []
    kv_args = []
    for blk in blocks:
        kv_specs.append(pl.BlockSpec((tok_rows, HEAD_WIDTH), lambda g: (0, g)))
        kv_specs.append(pl.BlockSpec((tok_rows, HEAD_WIDTH), lambda g, n=kv_heads: (0, n + g)))
        kv_specs.append(pl.BlockSpec((tok_rows, HEAD_WIDTH), lambda g, n=kv_heads: (0, 2 * n)))
        kv_args += [blk, blk, blk]
    return pl.pallas_call(
        band_kernel,
        grid=(kv_heads,),
        in_specs=[
            pl.BlockSpec((tok_rows, group_width), lambda g: (0, g)),
            pl.BlockSpec((tok_rows, group_width), lambda g: (0, g)),
        ]
        + kv_specs,
        out_specs=[
            pl.BlockSpec((tok_rows, group_width), lambda g: (0, g)),
            pl.BlockSpec((2, 2, tok_rows, HEAD_WIDTH), lambda g: (0, 0, 0, g)),
            pl.BlockSpec((2, tok_rows, HEAD_WIDTH), lambda g: (0, 0, g)),
            pl.BlockSpec((2, tok_rows, HEAD_WIDTH), lambda g: (0, 0, g)),
        ],
        out_shape=[
            jax.ShapeDtypeStruct((tok_rows, q_width), jnp.bfloat16),
            jax.ShapeDtypeStruct((2, 2, tok_rows, kv_width), jnp.bfloat16),
            jax.ShapeDtypeStruct((2, tok_rows, kv_width), jnp.float32),
            jax.ShapeDtypeStruct((2, tok_rows, kv_width), jnp.float32),
        ],
    )(query_blk, grad_blk, *kv_args)


def body(query_rows, key_rows, value_matrix, out_grad, segments):
    tok_rows = query_rows.shape[0]
    kv_width = key_rows.shape[1]
    kv_heads = kv_width // HEAD_WIDTH
    axes = ("ctx", "fsdp")
    seg_cols = jnp.broadcast_to(segments.astype(jnp.bfloat16)[:, None], (tok_rows, HEAD_WIDTH))
    own = jnp.concatenate([key_rows, value_matrix, seg_cols], 1)
    back_one = from_behind(own, axes, 1)
    back_two = from_behind(own, axes, 2)
    back_three = from_behind(back_two, axes, 1)
    blocks = [back_three, back_two, back_one, own]
    dq_part, send, middle, own_part = band_grads(query_rows, out_grad, blocks, kv_heads)
    received = from_behind(send, axes, -1)
    forward = (middle + received[0].astype(jnp.float32)).astype(jnp.bfloat16)
    gathered = from_behind(forward, axes, -2)
    total = own_part + received[1].astype(jnp.float32) + gathered.astype(jnp.float32)
    return (
        dq_part,
        total[0].astype(jnp.bfloat16),
        total[1].astype(jnp.bfloat16),
    )


def solution(mesh):
    return jax.shard_map(
        body,
        mesh=mesh,
        in_specs=(
            P(("ctx", "fsdp"), None),
            P(("ctx", "fsdp"), None),
            P(("ctx", "fsdp"), None),
            P(("ctx", "fsdp"), None),
            P(("ctx", "fsdp")),
        ),
        out_specs=(P(("ctx", "fsdp"), None), P(("ctx", "fsdp"), None), P(("ctx", "fsdp"), None)),
        check_vma=False,
    )
```

```python
import math

import jax
import jax.numpy as jnp
from jax import lax
from jax.experimental import pallas as pl
from jax.sharding import PartitionSpec as P

HEAD_WIDTH = 128
SPAN = 3


def from_behind(block, axis, distance):
    devices = range(lax.axis_size(axis))
    route = [(i - distance, i) for i in devices if i - distance in devices]
    return lax.ppermute(block, axis, route)


def band_kernel(query_ref, grad_ref, *refs):
    key_refs = refs[0:12:3]
    value_refs = refs[1:12:3]
    seg_refs = refs[2:12:3]
    dq_ref, send_ref, middle_ref, own_ref = refs[12:]
    tok_rows = query_ref.shape[0]
    key_count = tok_rows * len(key_refs)
    heads_per_group = query_ref.shape[1] // HEAD_WIDTH
    inv_root = 1.0 / math.sqrt(HEAD_WIDTH)
    window = key_count - tok_rows
    position = lax.axis_index(("ctx", "fsdp"))
    seg_q = seg_refs[-1][:, 0:1].astype(jnp.float32)
    seg_k = jnp.concatenate(
        [jnp.transpose(ref[...].astype(jnp.float32))[0:1] for ref in seg_refs], 1
    )
    row = lax.broadcasted_iota(jnp.int32, (tok_rows, key_count), 0)
    col = lax.broadcasted_iota(jnp.int32, (tok_rows, key_count), 1)
    allowed = (col > row) & (col <= row + window) & (col >= window - position * tok_rows)
    allowed = allowed & (seg_k == seg_q)
    k_head = jnp.concatenate([ref[...] for ref in key_refs], 0)
    v_head = jnp.concatenate([ref[...] for ref in value_refs], 0)
    key_acc = jnp.zeros((key_count, HEAD_WIDTH), jnp.float32)
    value_acc = jnp.zeros((key_count, HEAD_WIDTH), jnp.float32)
    def head_scores(head):
        cols = slice(head * HEAD_WIDTH, (head + 1) * HEAD_WIDTH)
        q_head = query_ref[:, cols]
        o_grad = grad_ref[:, cols]
        scores = lax.dot_general(
            q_head, k_head, (((1,), (1,)), ((), ())), preferred_element_type=jnp.float32
        )
        prob_grad = lax.dot_general(
            o_grad, v_head, (((1,), (1,)), ((), ())), preferred_element_type=jnp.float32
        )
        return q_head, o_grad, scores, prob_grad

    pending = head_scores(0)
    for head in range(heads_per_group):
        cols = slice(head * HEAD_WIDTH, (head + 1) * HEAD_WIDTH)
        q_head, o_grad, scores, prob_grad = pending
        if head + 1 < heads_per_group:
            pending = head_scores(head + 1)
        scores = jnp.where(allowed, scores * inv_root, -1e30)
        row_max = jnp.max(scores, axis=1, keepdims=True)
        weights = jnp.exp(scores - row_max)
        probs = weights * (1.0 / jnp.sum(weights, axis=1, keepdims=True))
        row_delta = jnp.sum(probs * prob_grad, axis=1, keepdims=True)
        score_grad = (probs * (prob_grad - row_delta) * inv_root).astype(jnp.bfloat16)
        probs_low = probs.astype(jnp.bfloat16)
        dq_ref[:, cols] = jnp.dot(
            score_grad, k_head, preferred_element_type=jnp.float32
        ).astype(jnp.bfloat16)
        key_acc = key_acc + lax.dot_general(
            score_grad, q_head, (((0,), (0,)), ((), ())), preferred_element_type=jnp.float32
        )
        value_acc = value_acc + lax.dot_general(
            probs_low, o_grad, (((0,), (0,)), ((), ())), preferred_element_type=jnp.float32
        )

    def rows(block):
        return slice(block * tok_rows, (block + 1) * tok_rows)

    for slot, block in enumerate((0, 2)):
        send_ref[slot, 0] = key_acc[rows(block)].astype(jnp.bfloat16)
        send_ref[slot, 1] = value_acc[rows(block)].astype(jnp.bfloat16)
    middle_ref[0] = key_acc[rows(1)]
    middle_ref[1] = value_acc[rows(1)]
    own_ref[0] = key_acc[rows(3)]
    own_ref[1] = value_acc[rows(3)]


def band_grads(query_blk, grad_blk, blocks, kv_heads):
    tok_rows, q_width = query_blk.shape
    kv_width = kv_heads * HEAD_WIDTH
    group_width = q_width // kv_heads
    kv_specs = []
    kv_args = []
    for blk in blocks:
        kv_specs.append(pl.BlockSpec((tok_rows, HEAD_WIDTH), lambda g: (0, g)))
        kv_specs.append(pl.BlockSpec((tok_rows, HEAD_WIDTH), lambda g, n=kv_heads: (0, n + g)))
        kv_specs.append(pl.BlockSpec((tok_rows, HEAD_WIDTH), lambda g, n=kv_heads: (0, 2 * n)))
        kv_args += [blk, blk, blk]
    return pl.pallas_call(
        band_kernel,
        grid=(kv_heads,),
        in_specs=[
            pl.BlockSpec((tok_rows, group_width), lambda g: (0, g)),
            pl.BlockSpec((tok_rows, group_width), lambda g: (0, g)),
        ]
        + kv_specs,
        out_specs=[
            pl.BlockSpec((tok_rows, group_width), lambda g: (0, g)),
            pl.BlockSpec((2, 2, tok_rows, HEAD_WIDTH), lambda g: (0, 0, 0, g)),
            pl.BlockSpec((2, tok_rows, HEAD_WIDTH), lambda g: (0, 0, g)),
            pl.BlockSpec((2, tok_rows, HEAD_WIDTH), lambda g: (0, 0, g)),
        ],
        out_shape=[
            jax.ShapeDtypeStruct((tok_rows, q_width), jnp.bfloat16),
            jax.ShapeDtypeStruct((2, 2, tok_rows, kv_width), jnp.bfloat16),
            jax.ShapeDtypeStruct((2, tok_rows, kv_width), jnp.float32),
            jax.ShapeDtypeStruct((2, tok_rows, kv_width), jnp.float32),
        ],
    )(query_blk, grad_blk, *kv_args)


def body(query_rows, key_rows, value_matrix, out_grad, segments):
    tok_rows = query_rows.shape[0]
    kv_width = key_rows.shape[1]
    kv_heads = kv_width // HEAD_WIDTH
    axes = ("ctx", "fsdp")
    seg_cols = jnp.broadcast_to(segments.astype(jnp.bfloat16)[:, None], (tok_rows, HEAD_WIDTH))
    own = jnp.concatenate([key_rows, value_matrix, seg_cols], 1)
    back_one = from_behind(own, axes, 1)
    back_two = from_behind(own, axes, 2)
    back_three = from_behind(back_two, axes, 1)
    blocks = [back_three, back_two, back_one, own]
    dq_part, send, middle, own_part = band_grads(query_rows, out_grad, blocks, kv_heads)
    received = from_behind(send, axes, -1)
    forward = (middle + received[0].astype(jnp.float32)).astype(jnp.bfloat16)
    gathered = from_behind(forward, axes, -2)
    total = own_part + received[1].astype(jnp.float32) + gathered.astype(jnp.float32)
    return (
        dq_part,
        total[0].astype(jnp.bfloat16),
        total[1].astype(jnp.bfloat16),
    )


def solution(mesh):
    return jax.shard_map(
        body,
        mesh=mesh,
        in_specs=(
            P(("ctx", "fsdp"), None),
            P(("ctx", "fsdp"), None),
            P(("ctx", "fsdp"), None),
            P(("ctx", "fsdp"), None),
            P(("ctx", "fsdp")),
        ),
        out_specs=(P(("ctx", "fsdp"), None), P(("ctx", "fsdp"), None), P(("ctx", "fsdp"), None)),
        check_vma=False,
    )
```

```python
import math

import jax
import jax.numpy as jnp
from jax import lax
from jax.experimental import pallas as pl
from jax.sharding import PartitionSpec as P

HEAD_WIDTH = 128
SPAN = 3


def from_behind(block, axis, distance):
    devices = range(lax.axis_size(axis))
    route = [(i - distance, i) for i in devices if i - distance in devices]
    return lax.ppermute(block, axis, route)


def band_kernel(query_ref, grad_ref, *refs):
    key_refs = refs[0:12:3]
    value_refs = refs[1:12:3]
    seg_refs = refs[2:12:3]
    dq_ref, send_ref, middle_ref, own_ref = refs[12:]
    tok_rows = query_ref.shape[0]
    key_count = tok_rows * len(key_refs)
    heads_per_group = query_ref.shape[1] // HEAD_WIDTH
    inv_root = 1.0 / math.sqrt(HEAD_WIDTH)
    window = key_count - tok_rows
    position = lax.axis_index(("ctx", "fsdp"))
    seg_q = seg_refs[-1][:, 0:1].astype(jnp.float32)
    seg_k = jnp.concatenate(
        [jnp.transpose(ref[...].astype(jnp.float32))[0:1] for ref in seg_refs], 1
    )
    row = lax.broadcasted_iota(jnp.int32, (tok_rows, key_count), 0)
    col = lax.broadcasted_iota(jnp.int32, (tok_rows, key_count), 1)
    allowed = (col > row) & (col <= row + window) & (col >= window - position * tok_rows)
    allowed = allowed & (seg_k == seg_q)
    k_head = jnp.concatenate([ref[...] for ref in key_refs], 0)
    v_head = jnp.concatenate([ref[...] for ref in value_refs], 0)
    key_acc = jnp.zeros((key_count, HEAD_WIDTH), jnp.float32)
    value_acc = jnp.zeros((key_count, HEAD_WIDTH), jnp.float32)
    def head_scores(head):
        cols = slice(head * HEAD_WIDTH, (head + 1) * HEAD_WIDTH)
        q_head = query_ref[:, cols]
        o_grad = grad_ref[:, cols]
        scores = lax.dot_general(
            q_head, k_head, (((1,), (1,)), ((), ())), preferred_element_type=jnp.float32
        )
        prob_grad = lax.dot_general(
            o_grad, v_head, (((1,), (1,)), ((), ())), preferred_element_type=jnp.float32
        )
        return q_head, o_grad, scores, prob_grad

    pending = head_scores(0)
    for head in range(heads_per_group):
        cols = slice(head * HEAD_WIDTH, (head + 1) * HEAD_WIDTH)
        q_head, o_grad, scores, prob_grad = pending
        if head + 1 < heads_per_group:
            pending = head_scores(head + 1)
        scores = jnp.where(allowed, scores * inv_root, -1e30)
        row_max = jnp.max(scores, axis=1, keepdims=True)
        weights = jnp.exp(scores - row_max)
        probs = weights * (1.0 / jnp.sum(weights, axis=1, keepdims=True))
        row_delta = jnp.sum(probs * prob_grad, axis=1, keepdims=True)
        score_grad = (probs * (prob_grad - row_delta) * inv_root).astype(jnp.bfloat16)
        probs_low = probs.astype(jnp.bfloat16)
        dq_ref[:, cols] = jnp.dot(
            score_grad, k_head, preferred_element_type=jnp.float32
        ).astype(jnp.bfloat16)
        key_acc = key_acc + lax.dot_general(
            score_grad, q_head, (((0,), (0,)), ((), ())), preferred_element_type=jnp.float32
        )
        value_acc = value_acc + lax.dot_general(
            probs_low, o_grad, (((0,), (0,)), ((), ())), preferred_element_type=jnp.float32
        )

    def rows(block):
        return slice(block * tok_rows, (block + 1) * tok_rows)

    for slot, block in enumerate((0, 2)):
        send_ref[slot, 0] = key_acc[rows(block)].astype(jnp.bfloat16)
        send_ref[slot, 1] = value_acc[rows(block)].astype(jnp.bfloat16)
    middle_ref[0] = key_acc[rows(1)]
    middle_ref[1] = value_acc[rows(1)]
    own_ref[0] = key_acc[rows(3)]
    own_ref[1] = value_acc[rows(3)]


def band_grads(query_blk, grad_blk, blocks, kv_heads):
    tok_rows, q_width = query_blk.shape
    kv_width = kv_heads * HEAD_WIDTH
    group_width = q_width // kv_heads
    kv_specs = []
    kv_args = []
    for blk in blocks:
        kv_specs.append(pl.BlockSpec((tok_rows, HEAD_WIDTH), lambda g: (0, g)))
        kv_specs.append(pl.BlockSpec((tok_rows, HEAD_WIDTH), lambda g, n=kv_heads: (0, n + g)))
        kv_specs.append(pl.BlockSpec((tok_rows, HEAD_WIDTH), lambda g, n=kv_heads: (0, 2 * n)))
        kv_args += [blk, blk, blk]
    return pl.pallas_call(
        band_kernel,
        grid=(kv_heads,),
        in_specs=[
            pl.BlockSpec((tok_rows, group_width), lambda g: (0, g)),
            pl.BlockSpec((tok_rows, group_width), lambda g: (0, g)),
        ]
        + kv_specs,
        out_specs=[
            pl.BlockSpec((tok_rows, group_width), lambda g: (0, g)),
            pl.BlockSpec((2, 2, tok_rows, HEAD_WIDTH), lambda g: (0, 0, 0, g)),
            pl.BlockSpec((2, tok_rows, HEAD_WIDTH), lambda g: (0, 0, g)),
            pl.BlockSpec((2, tok_rows, HEAD_WIDTH), lambda g: (0, 0, g)),
        ],
        out_shape=[
            jax.ShapeDtypeStruct((tok_rows, q_width), jnp.bfloat16),
            jax.ShapeDtypeStruct((2, 2, tok_rows, kv_width), jnp.bfloat16),
            jax.ShapeDtypeStruct((2, tok_rows, kv_width), jnp.float32),
            jax.ShapeDtypeStruct((2, tok_rows, kv_width), jnp.float32),
        ],
    )(query_blk, grad_blk, *kv_args)


def body(query_rows, key_rows, value_matrix, out_grad, segments):
    tok_rows = query_rows.shape[0]
    kv_width = key_rows.shape[1]
    kv_heads = kv_width // HEAD_WIDTH
    axes = ("ctx", "fsdp")
    seg_cols = jnp.broadcast_to(segments.astype(jnp.bfloat16)[:, None], (tok_rows, HEAD_WIDTH))
    own = jnp.concatenate([key_rows, value_matrix, seg_cols], 1)
    back_one = from_behind(own, axes, 1)
    back_two = from_behind(back_one, axes, 1)
    back_three = from_behind(back_two, axes, 1)
    blocks = [back_three, back_two, back_one, own]
    dq_part, send, middle, own_part = band_grads(query_rows, out_grad, blocks, kv_heads)
    received = from_behind(send, axes, -1)
    forward = (middle + received[0].astype(jnp.float32)).astype(jnp.bfloat16)
    gathered = from_behind(forward, axes, -2)
    total = own_part + received[1].astype(jnp.float32) + gathered.astype(jnp.float32)
    return (
        dq_part,
        total[0].astype(jnp.bfloat16),
        total[1].astype(jnp.bfloat16),
    )


def solution(mesh):
    return jax.shard_map(
        body,
        mesh=mesh,
        in_specs=(
            P(("ctx", "fsdp"), None),
            P(("ctx", "fsdp"), None),
            P(("ctx", "fsdp"), None),
            P(("ctx", "fsdp"), None),
            P(("ctx", "fsdp")),
        ),
        out_specs=(P(("ctx", "fsdp"), None), P(("ctx", "fsdp"), None), P(("ctx", "fsdp"), None)),
        check_vma=False,
    )
```

```python
import math

import jax
import jax.numpy as jnp
from jax import lax
from jax.experimental import pallas as pl
from jax.sharding import PartitionSpec as P

HEAD_WIDTH = 128
SPAN = 3
GROUP_HEADS = 8


def from_behind(block, axis, distance):
    devices = range(lax.axis_size(axis))
    route = [(i - distance, i) for i in devices if i - distance in devices]
    return lax.ppermute(block, axis, route)


def band_kernel(query_ref, grad_ref, *refs):
    key_refs = refs[0:12:3]
    value_refs = refs[1:12:3]
    seg_refs = refs[2:12:3]
    dq_ref, send_ref, middle_ref, own_ref = refs[-4:]
    tok_rows = query_ref.shape[0]
    key_count = tok_rows * len(key_refs)
    heads_per_group = query_ref.shape[1] // HEAD_WIDTH
    inv_root = 1.0 / math.sqrt(HEAD_WIDTH)
    window = key_count - tok_rows
    position = lax.axis_index(("ctx", "fsdp"))
    seg_q = seg_refs[-1][:, 0:1].astype(jnp.float32)
    seg_k = jnp.concatenate(
        [jnp.transpose(ref[...].astype(jnp.float32))[0:1] for ref in seg_refs], 1
    )
    row = lax.broadcasted_iota(jnp.int32, (tok_rows, key_count), 0)
    col = lax.broadcasted_iota(jnp.int32, (tok_rows, key_count), 1)
    allowed = (col > row) & (col <= row + window) & (col >= window - position * tok_rows)
    allowed = allowed & (seg_k == seg_q)
    k_head = jnp.concatenate([ref[...] for ref in key_refs], 0)
    v_head = jnp.concatenate([ref[...] for ref in value_refs], 0)
    key_acc = jnp.zeros((key_count, HEAD_WIDTH), jnp.float32)
    value_acc = jnp.zeros((key_count, HEAD_WIDTH), jnp.float32)
    def head_scores(head):
        cols = slice(head * HEAD_WIDTH, (head + 1) * HEAD_WIDTH)
        q_head = query_ref[:, cols]
        o_grad = grad_ref[:, cols]
        scores = lax.dot_general(
            q_head, k_head, (((1,), (1,)), ((), ())), preferred_element_type=jnp.float32
        )
        prob_grad = lax.dot_general(
            o_grad, v_head, (((1,), (1,)), ((), ())), preferred_element_type=jnp.float32
        )
        return q_head, o_grad, scores, prob_grad

    pending = head_scores(0)
    for head in range(heads_per_group):
        cols = slice(head * HEAD_WIDTH, (head + 1) * HEAD_WIDTH)
        q_head, o_grad, scores, prob_grad = pending
        if head + 1 < heads_per_group:
            pending = head_scores(head + 1)
        scores = jnp.where(allowed, scores * inv_root, -1e30)
        row_max = jnp.max(scores, axis=1, keepdims=True)
        weights = jnp.exp(scores - row_max)
        probs = weights * (1.0 / jnp.sum(weights, axis=1, keepdims=True))
        row_delta = jnp.sum(probs * prob_grad, axis=1, keepdims=True)
        score_grad = (probs * (prob_grad - row_delta) * inv_root).astype(jnp.bfloat16)
        probs_low = probs.astype(jnp.bfloat16)
        dq_ref[:, cols] = jnp.dot(
            score_grad, k_head, preferred_element_type=jnp.float32
        ).astype(jnp.bfloat16)
        key_acc = key_acc + lax.dot_general(
            score_grad, q_head, (((0,), (0,)), ((), ())), preferred_element_type=jnp.float32
        )
        value_acc = value_acc + lax.dot_general(
            probs_low, o_grad, (((0,), (0,)), ((), ())), preferred_element_type=jnp.float32
        )

    def rows(block):
        return slice(block * tok_rows, (block + 1) * tok_rows)

    for slot, block in enumerate((0, 2)):
        send_ref[slot, 0] = key_acc[rows(block)].astype(jnp.bfloat16)
        send_ref[slot, 1] = value_acc[rows(block)].astype(jnp.bfloat16)
    middle_ref[0] = key_acc[rows(1)]
    middle_ref[1] = value_acc[rows(1)]
    own_ref[0] = key_acc[rows(3)]
    own_ref[1] = value_acc[rows(3)]


def band_grads(query_blk, grad_blk, kv_blocks, seg_blocks, first_kv, kv_heads, dq_buf):
    tok_rows, q_width = query_blk.shape
    group_width = HEAD_WIDTH * GROUP_HEADS
    half_width = kv_heads * HEAD_WIDTH
    kv_specs = []
    kv_args = []
    for (blk, k_off, v_off), (seg_blk, seg_off) in zip(kv_blocks, seg_blocks):
        kv_specs.append(pl.BlockSpec((tok_rows, HEAD_WIDTH), lambda g, o=k_off: (0, o + g)))
        kv_specs.append(pl.BlockSpec((tok_rows, HEAD_WIDTH), lambda g, o=v_off: (0, o + g)))
        kv_specs.append(pl.BlockSpec((tok_rows, HEAD_WIDTH), lambda g, o=seg_off: (0, o)))
        kv_args += [blk, blk, seg_blk]
    extra_specs = []
    extra_args = []
    aliases = {}
    if dq_buf is not None:
        extra_specs = [pl.BlockSpec(memory_space=pl.ANY)]
        extra_args = [dq_buf]
        aliases = {2 + len(kv_args): 0}
    return pl.pallas_call(
        band_kernel,
        grid=(kv_heads,),
        in_specs=[
            pl.BlockSpec((tok_rows, group_width), lambda g, f=first_kv: (0, f + g)),
            pl.BlockSpec((tok_rows, group_width), lambda g, f=first_kv: (0, f + g)),
        ]
        + kv_specs
        + extra_specs,
        out_specs=[
            pl.BlockSpec((tok_rows, group_width), lambda g, f=first_kv: (0, f + g)),
            pl.BlockSpec((2, 2, tok_rows, HEAD_WIDTH), lambda g: (0, 0, 0, g)),
            pl.BlockSpec((2, tok_rows, HEAD_WIDTH), lambda g: (0, 0, g)),
            pl.BlockSpec((2, tok_rows, HEAD_WIDTH), lambda g: (0, 0, g)),
        ],
        out_shape=[
            jax.ShapeDtypeStruct((tok_rows, q_width), jnp.bfloat16),
            jax.ShapeDtypeStruct((2, 2, tok_rows, half_width), jnp.bfloat16),
            jax.ShapeDtypeStruct((2, tok_rows, half_width), jnp.float32),
            jax.ShapeDtypeStruct((2, tok_rows, half_width), jnp.float32),
        ],
        input_output_aliases=aliases,
    )(query_blk, grad_blk, *kv_args, *extra_args)


def body(query_rows, key_rows, value_matrix, out_grad, segments):
    tok_rows = query_rows.shape[0]
    kv_width = key_rows.shape[1]
    kv_heads = kv_width // HEAD_WIDTH
    half = kv_heads // 2
    w = HEAD_WIDTH
    axes = ("ctx", "fsdp")
    seg_cols = jnp.broadcast_to(segments.astype(jnp.bfloat16)[:, None], (tok_rows, HEAD_WIDTH))
    own = jnp.concatenate([key_rows, value_matrix, seg_cols], 1)
    back_one = from_behind(own, axes, 1)
    back_two = from_behind(own, axes, 2)
    seg_at = 2 * kv_heads
    two_first = jnp.concatenate(
        [
            back_two[:, 0 : half * w],
            back_two[:, kv_heads * w : (kv_heads + half) * w],
            back_two[:, seg_at * w : (seg_at + 1) * w],
        ],
        1,
    )
    two_second = jnp.concatenate(
        [back_two[:, half * w : kv_heads * w], back_two[:, (kv_heads + half) * w : seg_at * w]],
        1,
    )
    three_first = from_behind(two_first, axes, 1)
    three_second = from_behind(two_second, axes, 1)
    full = [(back_two, 0, kv_heads), (back_one, 0, kv_heads), (own, 0, kv_heads)]
    segs = [(back_two, seg_at), (back_one, seg_at), (own, seg_at)]
    dq_part, send_a, middle_a, own_a = band_grads(
        query_rows,
        out_grad,
        [(three_first, 0, half)] + full,
        [(three_first, 2 * half)] + segs,
        0,
        half,
        None,
    )
    dq_part, send_b, middle_b, own_b = band_grads(
        query_rows,
        out_grad,
        [(three_second, 0, half)] + [(b, k + half, v + half) for b, k, v in full],
        [(three_first, 2 * half)] + segs,
        half,
        half,
        dq_part,
    )
    received_a = from_behind(send_a, axes, -1)
    received_b = from_behind(send_b, axes, -1)
    forward = jnp.concatenate(
        [
            middle_a + received_a[0].astype(jnp.float32),
            middle_b + received_b[0].astype(jnp.float32),
        ],
        2,
    ).astype(jnp.bfloat16)
    gathered = from_behind(forward, axes, -2)
    total = jnp.concatenate(
        [
            own_a + received_a[1].astype(jnp.float32),
            own_b + received_b[1].astype(jnp.float32),
        ],
        2,
    ) + gathered.astype(jnp.float32)
    return (
        dq_part,
        total[0].astype(jnp.bfloat16),
        total[1].astype(jnp.bfloat16),
    )


def solution(mesh):
    return jax.shard_map(
        body,
        mesh=mesh,
        in_specs=(
            P(("ctx", "fsdp"), None),
            P(("ctx", "fsdp"), None),
            P(("ctx", "fsdp"), None),
            P(("ctx", "fsdp"), None),
            P(("ctx", "fsdp")),
        ),
        out_specs=(P(("ctx", "fsdp"), None), P(("ctx", "fsdp"), None), P(("ctx", "fsdp"), None)),
        check_vma=False,
    )
```

```python
import math

import jax
import jax.numpy as jnp
from jax import lax
from jax.experimental import pallas as pl
from jax.sharding import PartitionSpec as P

HEAD_WIDTH = 128
SPAN = 3


def from_behind(block, axis, distance):
    devices = range(lax.axis_size(axis))
    route = [(i - distance, i) for i in devices if i - distance in devices]
    return lax.ppermute(block, axis, route)


def band_kernel(query_ref, grad_ref, *refs):
    key_refs = refs[0:12:3]
    value_refs = refs[1:12:3]
    seg_refs = refs[2:12:3]
    dq_ref, send_ref, middle_ref, own_ref = refs[12:]
    tok_rows = query_ref.shape[0]
    key_count = tok_rows * len(key_refs)
    heads_per_group = query_ref.shape[1] // HEAD_WIDTH
    inv_root = 1.0 / math.sqrt(HEAD_WIDTH)
    window = key_count - tok_rows
    position = lax.axis_index(("ctx", "fsdp"))
    seg_q = seg_refs[-1][:, 0:1].astype(jnp.float32)
    seg_k = jnp.concatenate(
        [jnp.transpose(ref[...].astype(jnp.float32))[0:1] for ref in seg_refs], 1
    )
    row = lax.broadcasted_iota(jnp.int32, (tok_rows, key_count), 0)
    col = lax.broadcasted_iota(jnp.int32, (tok_rows, key_count), 1)
    allowed = (col > row) & (col <= row + window) & (col >= window - position * tok_rows)
    allowed = allowed & (seg_k == seg_q)
    k_head = jnp.concatenate([ref[...] for ref in key_refs], 0)
    v_head = jnp.concatenate([ref[...] for ref in value_refs], 0)
    key_acc_t = jnp.zeros((HEAD_WIDTH, key_count), jnp.float32)
    value_acc_t = jnp.zeros((HEAD_WIDTH, key_count), jnp.float32)
    def head_scores(head):
        cols = slice(head * HEAD_WIDTH, (head + 1) * HEAD_WIDTH)
        q_head = query_ref[:, cols]
        o_grad = grad_ref[:, cols]
        scores = lax.dot_general(
            q_head, k_head, (((1,), (1,)), ((), ())), preferred_element_type=jnp.float32
        )
        prob_grad = lax.dot_general(
            o_grad, v_head, (((1,), (1,)), ((), ())), preferred_element_type=jnp.float32
        )
        return jnp.transpose(q_head), jnp.transpose(o_grad), scores, prob_grad

    pending = head_scores(0)
    for head in range(heads_per_group):
        cols = slice(head * HEAD_WIDTH, (head + 1) * HEAD_WIDTH)
        q_head_t, o_grad_t, scores, prob_grad = pending
        if head + 1 < heads_per_group:
            pending = head_scores(head + 1)
        scores = jnp.where(allowed, scores * inv_root, -1e30)
        row_max = jnp.max(scores, axis=1, keepdims=True)
        weights = jnp.exp(scores - row_max)
        probs = weights * (1.0 / jnp.sum(weights, axis=1, keepdims=True))
        row_delta = jnp.sum(probs * prob_grad, axis=1, keepdims=True)
        score_grad = (probs * (prob_grad - row_delta) * inv_root).astype(jnp.bfloat16)
        probs_low = probs.astype(jnp.bfloat16)
        dq_ref[:, cols] = jnp.dot(
            score_grad, k_head, preferred_element_type=jnp.float32
        ).astype(jnp.bfloat16)
        key_acc_t = key_acc_t + jnp.dot(q_head_t, score_grad, preferred_element_type=jnp.float32)
        value_acc_t = value_acc_t + jnp.dot(
            o_grad_t, probs_low, preferred_element_type=jnp.float32
        )
    key_acc = jnp.transpose(key_acc_t)
    value_acc = jnp.transpose(value_acc_t)

    def rows(block):
        return slice(block * tok_rows, (block + 1) * tok_rows)

    for slot, block in enumerate((0, 2)):
        send_ref[slot, 0] = key_acc[rows(block)].astype(jnp.bfloat16)
        send_ref[slot, 1] = value_acc[rows(block)].astype(jnp.bfloat16)
    middle_ref[0] = key_acc[rows(1)]
    middle_ref[1] = value_acc[rows(1)]
    own_ref[0] = key_acc[rows(3)]
    own_ref[1] = value_acc[rows(3)]


def band_grads(query_blk, grad_blk, blocks, kv_heads):
    tok_rows, q_width = query_blk.shape
    kv_width = kv_heads * HEAD_WIDTH
    group_width = q_width // kv_heads
    kv_specs = []
    kv_args = []
    for blk in blocks:
        kv_specs.append(pl.BlockSpec((tok_rows, HEAD_WIDTH), lambda g: (0, g)))
        kv_specs.append(pl.BlockSpec((tok_rows, HEAD_WIDTH), lambda g, n=kv_heads: (0, n + g)))
        kv_specs.append(pl.BlockSpec((tok_rows, HEAD_WIDTH), lambda g, n=kv_heads: (0, 2 * n)))
        kv_args += [blk, blk, blk]
    return pl.pallas_call(
        band_kernel,
        grid=(kv_heads,),
        in_specs=[
            pl.BlockSpec((tok_rows, group_width), lambda g: (0, g)),
            pl.BlockSpec((tok_rows, group_width), lambda g: (0, g)),
        ]
        + kv_specs,
        out_specs=[
            pl.BlockSpec((tok_rows, group_width), lambda g: (0, g)),
            pl.BlockSpec((2, 2, tok_rows, HEAD_WIDTH), lambda g: (0, 0, 0, g)),
            pl.BlockSpec((2, tok_rows, HEAD_WIDTH), lambda g: (0, 0, g)),
            pl.BlockSpec((2, tok_rows, HEAD_WIDTH), lambda g: (0, 0, g)),
        ],
        out_shape=[
            jax.ShapeDtypeStruct((tok_rows, q_width), jnp.bfloat16),
            jax.ShapeDtypeStruct((2, 2, tok_rows, kv_width), jnp.bfloat16),
            jax.ShapeDtypeStruct((2, tok_rows, kv_width), jnp.float32),
            jax.ShapeDtypeStruct((2, tok_rows, kv_width), jnp.float32),
        ],
    )(query_blk, grad_blk, *kv_args)


def body(query_rows, key_rows, value_matrix, out_grad, segments):
    tok_rows = query_rows.shape[0]
    kv_width = key_rows.shape[1]
    kv_heads = kv_width // HEAD_WIDTH
    axes = ("ctx", "fsdp")
    seg_cols = jnp.broadcast_to(segments.astype(jnp.bfloat16)[:, None], (tok_rows, HEAD_WIDTH))
    own = jnp.concatenate([key_rows, value_matrix, seg_cols], 1)
    back_one = from_behind(own, axes, 1)
    back_two = from_behind(own, axes, 2)
    back_three = from_behind(back_two, axes, 1)
    blocks = [back_three, back_two, back_one, own]
    dq_part, send, middle, own_part = band_grads(query_rows, out_grad, blocks, kv_heads)
    received = from_behind(send, axes, -1)
    forward = (middle + received[0].astype(jnp.float32)).astype(jnp.bfloat16)
    gathered = from_behind(forward, axes, -2)
    total = own_part + received[1].astype(jnp.float32) + gathered.astype(jnp.float32)
    return (
        dq_part,
        total[0].astype(jnp.bfloat16),
        total[1].astype(jnp.bfloat16),
    )


def solution(mesh):
    return jax.shard_map(
        body,
        mesh=mesh,
        in_specs=(
            P(("ctx", "fsdp"), None),
            P(("ctx", "fsdp"), None),
            P(("ctx", "fsdp"), None),
            P(("ctx", "fsdp"), None),
            P(("ctx", "fsdp")),
        ),
        out_specs=(P(("ctx", "fsdp"), None), P(("ctx", "fsdp"), None), P(("ctx", "fsdp"), None)),
        check_vma=False,
    )
```

```python
import math

import jax
import jax.numpy as jnp
from jax import lax
from jax.experimental import pallas as pl
from jax.sharding import PartitionSpec as P

HEAD_WIDTH = 128
SPAN = 3
KV_PER_STEP = 2


def from_behind(block, axis, distance):
    devices = range(lax.axis_size(axis))
    route = [(i - distance, i) for i in devices if i - distance in devices]
    return lax.ppermute(block, axis, route)


def band_kernel(query_ref, grad_ref, *refs):
    key_refs = refs[0:12:3]
    value_refs = refs[1:12:3]
    seg_refs = refs[2:12:3]
    dq_ref, send_ref, middle_ref, own_ref = refs[12:]
    tok_rows = query_ref.shape[0]
    key_count = tok_rows * len(key_refs)
    heads_per_group = query_ref.shape[1] // HEAD_WIDTH
    inv_root = 1.0 / math.sqrt(HEAD_WIDTH)
    window = key_count - tok_rows
    position = lax.axis_index(("ctx", "fsdp"))
    seg_q = seg_refs[-1][:, 0:1].astype(jnp.float32)
    seg_k = jnp.concatenate(
        [jnp.transpose(ref[...].astype(jnp.float32))[0:1] for ref in seg_refs], 1
    )
    row = lax.broadcasted_iota(jnp.int32, (tok_rows, key_count), 0)
    col = lax.broadcasted_iota(jnp.int32, (tok_rows, key_count), 1)
    allowed = (col > row) & (col <= row + window) & (col >= window - position * tok_rows)
    allowed = allowed & (seg_k == seg_q)
    k_all = jnp.concatenate([ref[...] for ref in key_refs], 0)
    v_all = jnp.concatenate([ref[...] for ref in value_refs], 0)
    kv_per_step = k_all.shape[1] // HEAD_WIDTH
    heads_per_kv = heads_per_group // kv_per_step
    k_heads = [k_all[:, i * HEAD_WIDTH : (i + 1) * HEAD_WIDTH] for i in range(kv_per_step)]
    v_heads = [v_all[:, i * HEAD_WIDTH : (i + 1) * HEAD_WIDTH] for i in range(kv_per_step)]
    key_accs = [jnp.zeros((HEAD_WIDTH, key_count), jnp.float32) for _ in range(kv_per_step)]
    value_accs = [jnp.zeros((HEAD_WIDTH, key_count), jnp.float32) for _ in range(kv_per_step)]
    def head_scores(head):
        cols = slice(head * HEAD_WIDTH, (head + 1) * HEAD_WIDTH)
        q_head = query_ref[:, cols]
        o_grad = grad_ref[:, cols]
        k_head = k_heads[head // heads_per_kv]
        v_head = v_heads[head // heads_per_kv]
        scores = lax.dot_general(
            q_head, k_head, (((1,), (1,)), ((), ())), preferred_element_type=jnp.float32
        )
        prob_grad = lax.dot_general(
            o_grad, v_head, (((1,), (1,)), ((), ())), preferred_element_type=jnp.float32
        )
        return jnp.transpose(q_head), jnp.transpose(o_grad), scores, prob_grad

    pending = head_scores(0)
    for head in range(heads_per_group):
        cols = slice(head * HEAD_WIDTH, (head + 1) * HEAD_WIDTH)
        q_head_t, o_grad_t, scores, prob_grad = pending
        kv = head // heads_per_kv
        k_head = k_heads[kv]
        if head + 1 < heads_per_group:
            pending = head_scores(head + 1)
        scores = jnp.where(allowed, scores * inv_root, -1e30)
        row_max = jnp.max(scores, axis=1, keepdims=True)
        weights = jnp.exp(scores - row_max)
        probs = weights * (1.0 / jnp.sum(weights, axis=1, keepdims=True))
        row_delta = jnp.sum(probs * prob_grad, axis=1, keepdims=True)
        score_grad = (probs * (prob_grad - row_delta) * inv_root).astype(jnp.bfloat16)
        probs_low = probs.astype(jnp.bfloat16)
        dq_ref[:, cols] = jnp.dot(
            score_grad, k_head, preferred_element_type=jnp.float32
        ).astype(jnp.bfloat16)
        key_accs[kv] = key_accs[kv] + jnp.dot(
            q_head_t, score_grad, preferred_element_type=jnp.float32
        )
        value_accs[kv] = value_accs[kv] + jnp.dot(
            o_grad_t, probs_low, preferred_element_type=jnp.float32
        )

    def rows(block):
        return slice(block * tok_rows, (block + 1) * tok_rows)

    for kv in range(kv_per_step):
        lanes = slice(kv * HEAD_WIDTH, (kv + 1) * HEAD_WIDTH)
        key_acc = jnp.transpose(key_accs[kv])
        value_acc = jnp.transpose(value_accs[kv])
        for slot, block in enumerate((0, 2)):
            send_ref[slot, 0, :, lanes] = key_acc[rows(block)].astype(jnp.bfloat16)
            send_ref[slot, 1, :, lanes] = value_acc[rows(block)].astype(jnp.bfloat16)
        middle_ref[0, :, lanes] = key_acc[rows(1)]
        middle_ref[1, :, lanes] = value_acc[rows(1)]
        own_ref[0, :, lanes] = key_acc[rows(3)]
        own_ref[1, :, lanes] = value_acc[rows(3)]


def band_grads(query_blk, grad_blk, blocks, kv_heads):
    tok_rows, q_width = query_blk.shape
    kv_width = kv_heads * HEAD_WIDTH
    steps = kv_heads // KV_PER_STEP
    step_width = KV_PER_STEP * HEAD_WIDTH
    group_width = q_width // steps
    kv_specs = []
    kv_args = []
    for blk in blocks:
        kv_specs.append(pl.BlockSpec((tok_rows, step_width), lambda g: (0, g)))
        kv_specs.append(pl.BlockSpec((tok_rows, step_width), lambda g, n=steps: (0, n + g)))
        kv_specs.append(pl.BlockSpec((tok_rows, HEAD_WIDTH), lambda g, n=kv_heads: (0, 2 * n)))
        kv_args += [blk, blk, blk]
    return pl.pallas_call(
        band_kernel,
        grid=(steps,),
        in_specs=[
            pl.BlockSpec((tok_rows, group_width), lambda g: (0, g)),
            pl.BlockSpec((tok_rows, group_width), lambda g: (0, g)),
        ]
        + kv_specs,
        out_specs=[
            pl.BlockSpec((tok_rows, group_width), lambda g: (0, g)),
            pl.BlockSpec((2, 2, tok_rows, step_width), lambda g: (0, 0, 0, g)),
            pl.BlockSpec((2, tok_rows, step_width), lambda g: (0, 0, g)),
            pl.BlockSpec((2, tok_rows, step_width), lambda g: (0, 0, g)),
        ],
        out_shape=[
            jax.ShapeDtypeStruct((tok_rows, q_width), jnp.bfloat16),
            jax.ShapeDtypeStruct((2, 2, tok_rows, kv_width), jnp.bfloat16),
            jax.ShapeDtypeStruct((2, tok_rows, kv_width), jnp.float32),
            jax.ShapeDtypeStruct((2, tok_rows, kv_width), jnp.float32),
        ],
    )(query_blk, grad_blk, *kv_args)


def body(query_rows, key_rows, value_matrix, out_grad, segments):
    tok_rows = query_rows.shape[0]
    kv_width = key_rows.shape[1]
    kv_heads = kv_width // HEAD_WIDTH
    axes = ("ctx", "fsdp")
    seg_cols = jnp.broadcast_to(segments.astype(jnp.bfloat16)[:, None], (tok_rows, HEAD_WIDTH))
    own = jnp.concatenate([key_rows, value_matrix, seg_cols], 1)
    back_one = from_behind(own, axes, 1)
    back_two = from_behind(own, axes, 2)
    back_three = from_behind(back_two, axes, 1)
    blocks = [back_three, back_two, back_one, own]
    dq_part, send, middle, own_part = band_grads(query_rows, out_grad, blocks, kv_heads)
    received = from_behind(send, axes, -1)
    forward = (middle + received[0].astype(jnp.float32)).astype(jnp.bfloat16)
    gathered = from_behind(forward, axes, -2)
    total = own_part + received[1].astype(jnp.float32) + gathered.astype(jnp.float32)
    return (
        dq_part,
        total[0].astype(jnp.bfloat16),
        total[1].astype(jnp.bfloat16),
    )


def solution(mesh):
    return jax.shard_map(
        body,
        mesh=mesh,
        in_specs=(
            P(("ctx", "fsdp"), None),
            P(("ctx", "fsdp"), None),
            P(("ctx", "fsdp"), None),
            P(("ctx", "fsdp"), None),
            P(("ctx", "fsdp")),
        ),
        out_specs=(P(("ctx", "fsdp"), None), P(("ctx", "fsdp"), None), P(("ctx", "fsdp"), None)),
        check_vma=False,
    )
```

```python
import math

import jax
import jax.numpy as jnp
from jax import lax
from jax.experimental import pallas as pl
from jax.sharding import PartitionSpec as P

HEAD_WIDTH = 128
SPAN = 3
KV_PER_STEP = 4


def from_behind(block, axis, distance):
    devices = range(lax.axis_size(axis))
    route = [(i - distance, i) for i in devices if i - distance in devices]
    return lax.ppermute(block, axis, route)


def band_kernel(query_ref, grad_ref, *refs):
    key_refs = refs[0:12:3]
    value_refs = refs[1:12:3]
    seg_refs = refs[2:12:3]
    dq_ref, send_ref, middle_ref, own_ref = refs[12:]
    tok_rows = query_ref.shape[0]
    key_count = tok_rows * len(key_refs)
    heads_per_group = query_ref.shape[1] // HEAD_WIDTH
    inv_root = 1.0 / math.sqrt(HEAD_WIDTH)
    window = key_count - tok_rows
    position = lax.axis_index(("ctx", "fsdp"))
    seg_q = seg_refs[-1][:, 0:1].astype(jnp.float32)
    seg_k = jnp.concatenate(
        [jnp.transpose(ref[...].astype(jnp.float32))[0:1] for ref in seg_refs], 1
    )
    row = lax.broadcasted_iota(jnp.int32, (tok_rows, key_count), 0)
    col = lax.broadcasted_iota(jnp.int32, (tok_rows, key_count), 1)
    allowed = (col > row) & (col <= row + window) & (col >= window - position * tok_rows)
    allowed = allowed & (seg_k == seg_q)
    k_all = jnp.concatenate([ref[...] for ref in key_refs], 0)
    v_all = jnp.concatenate([ref[...] for ref in value_refs], 0)
    kv_per_step = k_all.shape[1] // HEAD_WIDTH
    heads_per_kv = heads_per_group // kv_per_step
    k_heads = [k_all[:, i * HEAD_WIDTH : (i + 1) * HEAD_WIDTH] for i in range(kv_per_step)]
    v_heads = [v_all[:, i * HEAD_WIDTH : (i + 1) * HEAD_WIDTH] for i in range(kv_per_step)]
    key_accs = [jnp.zeros((HEAD_WIDTH, key_count), jnp.float32) for _ in range(kv_per_step)]
    value_accs = [jnp.zeros((HEAD_WIDTH, key_count), jnp.float32) for _ in range(kv_per_step)]
    def head_scores(head):
        cols = slice(head * HEAD_WIDTH, (head + 1) * HEAD_WIDTH)
        q_head = query_ref[:, cols]
        o_grad = grad_ref[:, cols]
        k_head = k_heads[head // heads_per_kv]
        v_head = v_heads[head // heads_per_kv]
        scores = lax.dot_general(
            q_head, k_head, (((1,), (1,)), ((), ())), preferred_element_type=jnp.float32
        )
        prob_grad = lax.dot_general(
            o_grad, v_head, (((1,), (1,)), ((), ())), preferred_element_type=jnp.float32
        )
        return jnp.transpose(q_head), jnp.transpose(o_grad), scores, prob_grad

    pending = head_scores(0)
    for head in range(heads_per_group):
        cols = slice(head * HEAD_WIDTH, (head + 1) * HEAD_WIDTH)
        q_head_t, o_grad_t, scores, prob_grad = pending
        kv = head // heads_per_kv
        k_head = k_heads[kv]
        if head + 1 < heads_per_group:
            pending = head_scores(head + 1)
        scores = jnp.where(allowed, scores * inv_root, -1e30)
        row_max = jnp.max(scores, axis=1, keepdims=True)
        weights = jnp.exp(scores - row_max)
        probs = weights * (1.0 / jnp.sum(weights, axis=1, keepdims=True))
        row_delta = jnp.sum(probs * prob_grad, axis=1, keepdims=True)
        score_grad = (probs * (prob_grad - row_delta) * inv_root).astype(jnp.bfloat16)
        probs_low = probs.astype(jnp.bfloat16)
        dq_ref[:, cols] = jnp.dot(
            score_grad, k_head, preferred_element_type=jnp.float32
        ).astype(jnp.bfloat16)
        key_accs[kv] = key_accs[kv] + jnp.dot(
            q_head_t, score_grad, preferred_element_type=jnp.float32
        )
        value_accs[kv] = value_accs[kv] + jnp.dot(
            o_grad_t, probs_low, preferred_element_type=jnp.float32
        )

    def rows(block):
        return slice(block * tok_rows, (block + 1) * tok_rows)

    for kv in range(kv_per_step):
        lanes = slice(kv * HEAD_WIDTH, (kv + 1) * HEAD_WIDTH)
        key_acc = jnp.transpose(key_accs[kv])
        value_acc = jnp.transpose(value_accs[kv])
        for slot, block in enumerate((0, 2)):
            send_ref[slot, 0, :, lanes] = key_acc[rows(block)].astype(jnp.bfloat16)
            send_ref[slot, 1, :, lanes] = value_acc[rows(block)].astype(jnp.bfloat16)
        middle_ref[0, :, lanes] = key_acc[rows(1)]
        middle_ref[1, :, lanes] = value_acc[rows(1)]
        own_ref[0, :, lanes] = key_acc[rows(3)]
        own_ref[1, :, lanes] = value_acc[rows(3)]


def band_grads(query_blk, grad_blk, blocks, kv_heads):
    tok_rows, q_width = query_blk.shape
    kv_width = kv_heads * HEAD_WIDTH
    steps = kv_heads // KV_PER_STEP
    step_width = KV_PER_STEP * HEAD_WIDTH
    group_width = q_width // steps
    kv_specs = []
    kv_args = []
    for blk in blocks:
        kv_specs.append(pl.BlockSpec((tok_rows, step_width), lambda g: (0, g)))
        kv_specs.append(pl.BlockSpec((tok_rows, step_width), lambda g, n=steps: (0, n + g)))
        kv_specs.append(pl.BlockSpec((tok_rows, HEAD_WIDTH), lambda g, n=kv_heads: (0, 2 * n)))
        kv_args += [blk, blk, blk]
    return pl.pallas_call(
        band_kernel,
        grid=(steps,),
        in_specs=[
            pl.BlockSpec((tok_rows, group_width), lambda g: (0, g)),
            pl.BlockSpec((tok_rows, group_width), lambda g: (0, g)),
        ]
        + kv_specs,
        out_specs=[
            pl.BlockSpec((tok_rows, group_width), lambda g: (0, g)),
            pl.BlockSpec((2, 2, tok_rows, step_width), lambda g: (0, 0, 0, g)),
            pl.BlockSpec((2, tok_rows, step_width), lambda g: (0, 0, g)),
            pl.BlockSpec((2, tok_rows, step_width), lambda g: (0, 0, g)),
        ],
        out_shape=[
            jax.ShapeDtypeStruct((tok_rows, q_width), jnp.bfloat16),
            jax.ShapeDtypeStruct((2, 2, tok_rows, kv_width), jnp.bfloat16),
            jax.ShapeDtypeStruct((2, tok_rows, kv_width), jnp.float32),
            jax.ShapeDtypeStruct((2, tok_rows, kv_width), jnp.float32),
        ],
    )(query_blk, grad_blk, *kv_args)


def body(query_rows, key_rows, value_matrix, out_grad, segments):
    tok_rows = query_rows.shape[0]
    kv_width = key_rows.shape[1]
    kv_heads = kv_width // HEAD_WIDTH
    axes = ("ctx", "fsdp")
    seg_cols = jnp.broadcast_to(segments.astype(jnp.bfloat16)[:, None], (tok_rows, HEAD_WIDTH))
    own = jnp.concatenate([key_rows, value_matrix, seg_cols], 1)
    back_one = from_behind(own, axes, 1)
    back_two = from_behind(own, axes, 2)
    back_three = from_behind(back_two, axes, 1)
    blocks = [back_three, back_two, back_one, own]
    dq_part, send, middle, own_part = band_grads(query_rows, out_grad, blocks, kv_heads)
    received = from_behind(send, axes, -1)
    forward = (middle + received[0].astype(jnp.float32)).astype(jnp.bfloat16)
    gathered = from_behind(forward, axes, -2)
    total = own_part + received[1].astype(jnp.float32) + gathered.astype(jnp.float32)
    return (
        dq_part,
        total[0].astype(jnp.bfloat16),
        total[1].astype(jnp.bfloat16),
    )


def solution(mesh):
    return jax.shard_map(
        body,
        mesh=mesh,
        in_specs=(
            P(("ctx", "fsdp"), None),
            P(("ctx", "fsdp"), None),
            P(("ctx", "fsdp"), None),
            P(("ctx", "fsdp"), None),
            P(("ctx", "fsdp")),
        ),
        out_specs=(P(("ctx", "fsdp"), None), P(("ctx", "fsdp"), None), P(("ctx", "fsdp"), None)),
        check_vma=False,
    )
```

```python
import math

import jax
import jax.numpy as jnp
from jax import lax
from jax.experimental import pallas as pl
from jax.sharding import PartitionSpec as P

HEAD_WIDTH = 128
SPAN = 3
KV_PER_STEP = 2


def from_behind(block, axis, distance):
    devices = range(lax.axis_size(axis))
    route = [(i - distance, i) for i in devices if i - distance in devices]
    return lax.ppermute(block, axis, route)


def band_kernel(query_ref, grad_ref, *refs):
    key_refs = refs[0:12:3]
    value_refs = refs[1:12:3]
    seg_refs = refs[2:12:3]
    dq_ref, send_ref, middle_ref, own_ref = refs[12:]
    tok_rows = query_ref.shape[0]
    key_count = tok_rows * len(key_refs)
    heads_per_group = query_ref.shape[1] // HEAD_WIDTH
    inv_root = 1.0 / math.sqrt(HEAD_WIDTH)
    window = key_count - tok_rows
    position = lax.axis_index(("ctx", "fsdp"))
    seg_q = seg_refs[-1][:, 0:1].astype(jnp.float32)
    seg_k = jnp.concatenate(
        [jnp.transpose(ref[...].astype(jnp.float32))[0:1] for ref in seg_refs], 1
    )
    row = lax.broadcasted_iota(jnp.int32, (tok_rows, key_count), 0)
    col = lax.broadcasted_iota(jnp.int32, (tok_rows, key_count), 1)
    allowed = (col > row) & (col <= row + window) & (col >= window - position * tok_rows)
    allowed = allowed & (seg_k == seg_q)
    bias = jnp.where(allowed, 0.0, -1e30).astype(jnp.float32)
    k_all = jnp.concatenate([ref[...] for ref in key_refs], 0)
    v_all = jnp.concatenate([ref[...] for ref in value_refs], 0)
    kv_per_step = k_all.shape[1] // HEAD_WIDTH
    heads_per_kv = heads_per_group // kv_per_step
    k_heads = [k_all[:, i * HEAD_WIDTH : (i + 1) * HEAD_WIDTH] for i in range(kv_per_step)]
    v_heads = [v_all[:, i * HEAD_WIDTH : (i + 1) * HEAD_WIDTH] for i in range(kv_per_step)]
    key_accs = [jnp.zeros((HEAD_WIDTH, key_count), jnp.float32) for _ in range(kv_per_step)]
    value_accs = [jnp.zeros((HEAD_WIDTH, key_count), jnp.float32) for _ in range(kv_per_step)]
    def head_scores(head):
        cols = slice(head * HEAD_WIDTH, (head + 1) * HEAD_WIDTH)
        q_head = query_ref[:, cols]
        o_grad = grad_ref[:, cols]
        k_head = k_heads[head // heads_per_kv]
        v_head = v_heads[head // heads_per_kv]
        scores = lax.dot_general(
            q_head, k_head, (((1,), (1,)), ((), ())), preferred_element_type=jnp.float32
        )
        prob_grad = lax.dot_general(
            o_grad, v_head, (((1,), (1,)), ((), ())), preferred_element_type=jnp.float32
        )
        return jnp.transpose(q_head), jnp.transpose(o_grad), scores, prob_grad

    pending = [head_scores(head) for head in range(2)]
    for head in range(heads_per_group):
        cols = slice(head * HEAD_WIDTH, (head + 1) * HEAD_WIDTH)
        q_head_t, o_grad_t, scores, prob_grad = pending.pop(0)
        kv = head // heads_per_kv
        k_head = k_heads[kv]
        if head + 2 < heads_per_group:
            pending.append(head_scores(head + 2))
        scores = scores * inv_root + bias
        row_max = jnp.max(scores, axis=1, keepdims=True)
        weights = jnp.exp(scores - row_max)
        probs = weights * (1.0 / jnp.sum(weights, axis=1, keepdims=True))
        row_delta = jnp.sum(probs * prob_grad, axis=1, keepdims=True)
        score_grad = (probs * (prob_grad - row_delta) * inv_root).astype(jnp.bfloat16)
        probs_low = probs.astype(jnp.bfloat16)
        dq_ref[:, cols] = jnp.dot(
            score_grad, k_head, preferred_element_type=jnp.float32
        ).astype(jnp.bfloat16)
        key_accs[kv] = key_accs[kv] + jnp.dot(
            q_head_t, score_grad, preferred_element_type=jnp.float32
        )
        value_accs[kv] = value_accs[kv] + jnp.dot(
            o_grad_t, probs_low, preferred_element_type=jnp.float32
        )

    def rows(block):
        return slice(block * tok_rows, (block + 1) * tok_rows)

    for kv in range(kv_per_step):
        lanes = slice(kv * HEAD_WIDTH, (kv + 1) * HEAD_WIDTH)
        key_acc = jnp.transpose(key_accs[kv])
        value_acc = jnp.transpose(value_accs[kv])
        for slot, block in enumerate((0, 2)):
            send_ref[slot, 0, :, lanes] = key_acc[rows(block)].astype(jnp.bfloat16)
            send_ref[slot, 1, :, lanes] = value_acc[rows(block)].astype(jnp.bfloat16)
        middle_ref[0, :, lanes] = key_acc[rows(1)]
        middle_ref[1, :, lanes] = value_acc[rows(1)]
        own_ref[0, :, lanes] = key_acc[rows(3)]
        own_ref[1, :, lanes] = value_acc[rows(3)]


def band_grads(query_blk, grad_blk, blocks, kv_heads):
    tok_rows, q_width = query_blk.shape
    kv_width = kv_heads * HEAD_WIDTH
    steps = kv_heads // KV_PER_STEP
    step_width = KV_PER_STEP * HEAD_WIDTH
    group_width = q_width // steps
    kv_specs = []
    kv_args = []
    for blk in blocks:
        kv_specs.append(pl.BlockSpec((tok_rows, step_width), lambda g: (0, g)))
        kv_specs.append(pl.BlockSpec((tok_rows, step_width), lambda g, n=steps: (0, n + g)))
        kv_specs.append(pl.BlockSpec((tok_rows, HEAD_WIDTH), lambda g, n=kv_heads: (0, 2 * n)))
        kv_args += [blk, blk, blk]
    return pl.pallas_call(
        band_kernel,
        grid=(steps,),
        in_specs=[
            pl.BlockSpec((tok_rows, group_width), lambda g: (0, g)),
            pl.BlockSpec((tok_rows, group_width), lambda g: (0, g)),
        ]
        + kv_specs,
        out_specs=[
            pl.BlockSpec((tok_rows, group_width), lambda g: (0, g)),
            pl.BlockSpec((2, 2, tok_rows, step_width), lambda g: (0, 0, 0, g)),
            pl.BlockSpec((2, tok_rows, step_width), lambda g: (0, 0, g)),
            pl.BlockSpec((2, tok_rows, step_width), lambda g: (0, 0, g)),
        ],
        out_shape=[
            jax.ShapeDtypeStruct((tok_rows, q_width), jnp.bfloat16),
            jax.ShapeDtypeStruct((2, 2, tok_rows, kv_width), jnp.bfloat16),
            jax.ShapeDtypeStruct((2, tok_rows, kv_width), jnp.float32),
            jax.ShapeDtypeStruct((2, tok_rows, kv_width), jnp.float32),
        ],
    )(query_blk, grad_blk, *kv_args)


def body(query_rows, key_rows, value_matrix, out_grad, segments):
    tok_rows = query_rows.shape[0]
    kv_width = key_rows.shape[1]
    kv_heads = kv_width // HEAD_WIDTH
    axes = ("ctx", "fsdp")
    seg_cols = jnp.broadcast_to(segments.astype(jnp.bfloat16)[:, None], (tok_rows, HEAD_WIDTH))
    own = jnp.concatenate([key_rows, value_matrix, seg_cols], 1)
    back_one = from_behind(own, axes, 1)
    back_two = from_behind(own, axes, 2)
    back_three = from_behind(back_two, axes, 1)
    blocks = [back_three, back_two, back_one, own]
    dq_part, send, middle, own_part = band_grads(query_rows, out_grad, blocks, kv_heads)
    received = from_behind(send, axes, -1)
    forward = (middle + received[0].astype(jnp.float32)).astype(jnp.bfloat16)
    gathered = from_behind(forward, axes, -2)
    total = own_part + received[1].astype(jnp.float32) + gathered.astype(jnp.float32)
    return (
        dq_part,
        total[0].astype(jnp.bfloat16),
        total[1].astype(jnp.bfloat16),
    )


def solution(mesh):
    return jax.shard_map(
        body,
        mesh=mesh,
        in_specs=(
            P(("ctx", "fsdp"), None),
            P(("ctx", "fsdp"), None),
            P(("ctx", "fsdp"), None),
            P(("ctx", "fsdp"), None),
            P(("ctx", "fsdp")),
        ),
        out_specs=(P(("ctx", "fsdp"), None), P(("ctx", "fsdp"), None), P(("ctx", "fsdp"), None)),
        check_vma=False,
    )
```
